512 devices in a mesh: tensor: 4 (over x), request: 128 (over z, y, core).
Axes of the slice: x: 4, y: 4, z: 16, core: 2. Of those that a mesh axis runs over, the one named last changes fastest.
Arguments:
- hidden: bfloat16 [1024, 2048], P('request'), may hold values from -6 to 6
- norm_gain: float32 [2048], replicated, may hold values from 0.1 to 1.9
- w_query: bfloat16 [2048, 2048], P(None, 'tensor'), may hold values from -0.125 to 0.125
- w_keyval: bfloat16 [2048, 512], P(None, 'tensor'), may hold values from -0.125 to 0.125
- w_output: bfloat16 [2048, 2048], P('tensor'), may hold values from -0.125 to 0.125
- node_cache: bfloat16 [128, 4, 512, 128], P('request', 'tensor'), may hold values from -300 to 300
- leaf_cache: bfloat16 [1024, 4, 128, 128], P('request', 'tensor'), may hold values from -300 to 300
- leaf_branch: int32 [1024], replicated, may hold values from 0 to 63
- branch_root: int32 [64], replicated, may hold values from 0 to 7
- root_owner: int32 [8], replicated, may hold values from 0 to 127, as said below
- branch_owner: int32 [64], replicated, may hold values from 1 to 126, as said below
- root_len: int32 [8], replicated, may hold values from 1 to 512, as said below
- branch_len: int32 [64], replicated, may hold values from 1 to 512, as said below
- leaf_len: int32 [1024], P('request'), may hold values from 0 to 127, as said below
Outputs:
- mixed: bfloat16 [1024, 2048], P('request', 'tensor')
- new_entries: bfloat16 [1024, 4, 128], P('request', 'tensor')
The draws below stay inside these ranges and needn't reach their ends.
Inputs may be any that keep to these rules, and one draw needn't show every extreme that they name: The 8 entries of root_owner are all different slots. `branch_owner`: different from every entry of root_owner and from one another. `root_len`: some root has exactly 512 positions. `branch_len`: some branch has exactly 512 positions. `leaf_len`: some leaf has exactly 127 positions.
All inputs are finite; a program needn't handle non-finite values.
Results may differ from the reference program's by a relative error of at most 0.029.
Values may be sent and summed in bfloat16 or wider, within the bound.
No kernel may reach another device: no remote copies, remote signals or barrier semaphores. Data moves between devices by JAX's collectives and lax.ppermute only.
A program may use at most 128 MiB of HBM per device.

```python
import math
import jax
import jax.numpy as jnp
import numpy as np
from jax import lax

D = 2048
KV_HEADS = 4
HEAD_DIM = 64
HEADS = 32
GROUP = 8
NODE_LEN = 512
LEAF_LEN = 128
LEAVES = 1024
ROOTS = 8
BRANCHES = 64
SLOTS = 128


def owner_table(key):
    key_middle = jax.random.fold_in(key, 5)
    key_roots = jax.random.fold_in(key, 6)
    key_branches = jax.random.fold_in(key, 7)
    middle = (2 + jax.random.permutation(key_middle, SLOTS - 4)).astype(jnp.int32)
    roots = jnp.concatenate([jnp.array([0, SLOTS - 1], jnp.int32), middle[:ROOTS - 2]])
    branches = jnp.concatenate([jnp.array([1, SLOTS - 2], jnp.int32), middle[ROOTS - 2:ROOTS + BRANCHES - 4]])
    roots = jnp.take(roots, jax.random.permutation(key_roots, ROOTS))
    branches = jnp.take(branches, jax.random.permutation(key_branches, BRANCHES))
    return (roots.astype(jnp.int32), branches.astype(jnp.int32))


def heavy_lengths(key, count, ceiling, lowest):
    key_level, key_value, key_place = jax.random.split(key, 3)
    level = jax.random.randint(key_level, (count,), 0, 4)
    limit = jnp.maximum(jnp.right_shift(jnp.full((count,), ceiling, jnp.int32), level), 1)
    values = lowest + jax.random.randint(key_value, (count,), 0, limit)
    spot = jax.random.randint(key_place, (), 0, count)
    return jnp.where(jnp.arange(count) == spot, lowest + ceiling - 1, values).astype(jnp.int32)


def cache_values(key, shape):
    key_base = jax.random.fold_in(key, 0)
    key_value = jax.random.fold_in(key, 2)
    lead = shape[:-1]
    half_dim = shape[-1] // 2
    key_rows = 2.0 * jnp.clip(jax.random.normal(key_base, lead + (half_dim,), jnp.float32), -6.0, 6.0)
    value_rows = jnp.clip(jax.random.normal(key_value, lead + (half_dim,), jnp.float32), -6.0, 6.0)
    return jnp.concatenate([key_rows, value_rows], -1)


def draw_root_owner(key, part):
    return owner_table(key)[0]


def draw_branch_owner(key, part):
    return owner_table(key)[1]


def draw_root_len(key, part):
    return heavy_lengths(jax.random.fold_in(key, 11), ROOTS, NODE_LEN, 1)


def draw_branch_len(key, part):
    return heavy_lengths(jax.random.fold_in(key, 12), BRANCHES, NODE_LEN, 1)


def draw_leaf_len(key, part):
    return heavy_lengths(jax.random.fold_in(key, 13), LEAVES, LEAF_LEN, 0)


def draw_node_cache(key, part):
    return cache_values(jax.random.fold_in(key, 21), (SLOTS, KV_HEADS, NODE_LEN, 2 * HEAD_DIM)).astype(jnp.bfloat16)


def draw_leaf_cache(key, part):
    return cache_values(jax.random.fold_in(key, 22), (LEAVES, KV_HEADS, LEAF_LEN, 2 * HEAD_DIM)).astype(jnp.bfloat16)


def plant(values, rng, low, top_value):
    index_at = [jax.random.randint(jax.random.fold_in(rng, axis), (), 0, length) for axis, length in enumerate(values.shape)]
    main_axis = values.shape.index(max(values.shape))
    beside = index_at[:main_axis] + [(index_at[main_axis] + 1) % values.shape[main_axis]] + index_at[main_axis + 1:]
    return values.at[tuple(index_at)].set(low).at[tuple(beside)].set(top_value)


def level_of(key, shape, cuts, smallest, top_value):
    def one(dim, blocks):
        heights = jax.random.uniform(jax.random.fold_in(jax.random.fold_in(key, 6), dim), (blocks,), jnp.float32, smallest / len(cuts), top_value / len(cuts))
        return jnp.repeat(jnp.exp(heights), shape[dim] // blocks).reshape((-1,) + (1,) * (len(shape) - dim - 1))

    loudness = one(*cuts[0])
    for cut in cuts[1:]:
        loudness = loudness * one(*cut)
    return loudness


def cumulative_ranks(amount, slope):
    portions = [(1 << 20) // math.isqrt(rank ** slope) + 1 for rank in range(1, amount + 1)]
    spread = 1 + sum(portions) // (1 << 30)
    return np.cumsum(np.array([max(1, weight // spread) for weight in portions]))


def skewed_ids(stream_key, shape, number_of, lean):
    grid = cumulative_ranks(number_of, lean)
    pick = jax.random.randint(jax.random.fold_in(stream_key, 1), shape, 0, int(grid[number_of - 1]))
    rank = jnp.searchsorted(jnp.asarray(grid, jnp.int32), pick, side="right")
    return jax.random.permutation(jax.random.fold_in(stream_key, 2), number_of)[rank].astype(jnp.int32)


def scatter_about(own_key, extent, width, bound, cuts=(), kind=jnp.bfloat16):
    drawn = width * jax.random.normal(own_key, extent, jnp.float32)
    if cuts:
        drawn = drawn * level_of(own_key, extent, cuts, -0.22, 0.18)
    return jnp.clip(drawn, -bound, bound).astype(kind)


def setup_inputs(seed: int = 0) -> dict:
    key_of = jax.random.split(jax.random.key(seed), 15)
    hidden = scatter_about(key_of[0], (LEAVES, D), 1.0, 6.0, ((0, 128),))
    norm_gain = jnp.clip(1.0 + 0.18 * jax.random.normal(key_of[1], (D,), jnp.float32), 0.1, 1.9)
    w_query = scatter_about(key_of[2], (D, HEADS * HEAD_DIM), D ** -0.5, 0.125, ((1, 4),))
    w_keyval = scatter_about(key_of[3], (D, KV_HEADS * 2 * HEAD_DIM), D ** -0.5, 0.125, ((1, 4),))
    w_output = scatter_about(key_of[4], (HEADS * HEAD_DIM, D), (HEADS * HEAD_DIM) ** -0.5, 0.125, ((0, 4),))
    node_cache = draw_node_cache(jax.random.fold_in(key_of[14], 71), 0)
    leaf_cache = draw_leaf_cache(jax.random.fold_in(key_of[14], 71), 0)
    leaf_branch = plant(skewed_ids(key_of[7], (LEAVES,), BRANCHES, 2), jax.random.fold_in(key_of[7], 3), 0, BRANCHES - 1).astype(jnp.int32)
    branch_root = plant(skewed_ids(key_of[8], (BRANCHES,), ROOTS, 1), jax.random.fold_in(key_of[8], 3), 0, ROOTS - 1).astype(jnp.int32)
    root_owner = draw_root_owner(jax.random.fold_in(key_of[14], 71), 0)
    branch_owner = draw_branch_owner(jax.random.fold_in(key_of[14], 71), 0)
    root_len = draw_root_len(jax.random.fold_in(key_of[14], 71), 0)
    branch_len = draw_branch_len(jax.random.fold_in(key_of[14], 71), 0)
    leaf_len = draw_leaf_len(jax.random.fold_in(key_of[14], 71), 0)
    return dict(hidden=hidden, norm_gain=norm_gain, w_query=w_query, w_keyval=w_keyval, w_output=w_output, node_cache=node_cache, leaf_cache=leaf_cache, leaf_branch=leaf_branch, branch_root=branch_root, root_owner=root_owner, branch_owner=branch_owner, root_len=root_len, branch_len=branch_len, leaf_len=leaf_len)


FLOOR = -1e+30

def rotate(values_in, positions):
    half_dim = values_in.shape[-1] // 2
    inverse_freq = 10000.0 ** (-(jnp.arange(half_dim, dtype=jnp.float32) * 2.0 / values_in.shape[-1]))
    angles = positions.astype(jnp.float32)[..., None] * inverse_freq
    angles = jnp.concatenate([angles, angles], -1)
    turned = jnp.concatenate([-values_in[..., half_dim:], values_in[..., :half_dim]], -1)
    return values_in * jnp.cos(angles) + turned * jnp.sin(angles)

def part_of(query_rows, cache_rows, length):
    factor = HEAD_DIM ** (-0.5)
    scores = jnp.einsum('hgd,hkd->hgk', query_rows.astype(jnp.float32), cache_rows[..., :HEAD_DIM].astype(jnp.float32)) * factor
    usable = (jnp.arange(cache_rows.shape[1], dtype=jnp.int32) < length)[None, None, :]
    scores = jnp.where(usable, scores, FLOOR)
    peak = lax.optimization_barrier(jnp.max(scores, -1))
    weights = jnp.where(usable, jnp.exp(scores - peak[..., None]), 0.0).astype(jnp.bfloat16)
    summed = jnp.einsum('hgk,hkd->hgd', weights.astype(jnp.float32), cache_rows[..., HEAD_DIM:].astype(jnp.float32))
    weight_sum = lax.optimization_barrier(jnp.sum(weights.astype(jnp.float32), -1))
    return (summed, weight_sum, peak)

def reference(hidden, norm_gain, w_query, w_keyval, w_output, node_cache, leaf_cache, leaf_branch, branch_root, root_owner, branch_owner, root_len, branch_len, leaf_len):
    widened = hidden.astype(jnp.float32)
    normed = (widened * lax.rsqrt(lax.optimization_barrier(jnp.mean(widened * widened, -1, keepdims=True)) + 1e-05) * norm_gain).astype(jnp.bfloat16)
    leaf_root = branch_root[leaf_branch]
    positions = root_len[leaf_root] + branch_len[leaf_branch] + leaf_len
    raw_query = jnp.dot(normed, w_query, preferred_element_type=jnp.float32).reshape(LEAVES, KV_HEADS, GROUP, HEAD_DIM)
    queries = rotate(raw_query, positions[:, None, None]).astype(jnp.bfloat16)
    raw_entry = jnp.dot(normed, w_keyval, preferred_element_type=jnp.float32).reshape(LEAVES, KV_HEADS, 2 * HEAD_DIM)
    new_entries = jnp.concatenate([rotate(raw_entry[..., :HEAD_DIM], positions[:, None]), raw_entry[..., HEAD_DIM:]], -1).astype(jnp.bfloat16)

    def one_leaf(leaf_index):
        branch = leaf_branch[leaf_index]
        root_id = branch_root[branch]
        own_query = queries[leaf_index]
        length = leaf_len[leaf_index]
        marker = (jnp.arange(leaf_cache.shape[2], dtype=jnp.int32) == length)[None, :, None]
        appended = jnp.where(marker, new_entries[leaf_index][:, None, :], leaf_cache[leaf_index])
        pieces = [part_of(own_query, node_cache[root_owner[root_id]], root_len[root_id]), part_of(own_query, node_cache[branch_owner[branch]], branch_len[branch]), part_of(own_query, appended, length + 1)]
        peak = jnp.maximum(jnp.maximum(pieces[0][2], pieces[1][2]), pieces[2][2])
        numerator = jnp.zeros(peak.shape + (HEAD_DIM,), jnp.float32)
        denominator = jnp.zeros(peak.shape, jnp.float32)
        for summed, weight_sum, part_peak in pieces:
            scaled = jnp.exp(part_peak - peak)
            numerator = numerator + scaled[..., None] * summed
            denominator = denominator + scaled * weight_sum
        return (numerator / denominator[..., None]).astype(jnp.bfloat16)
    attended = lax.map(one_leaf, jnp.arange(LEAVES, dtype=jnp.int32)).reshape(LEAVES, HEADS * HEAD_DIM)
    mixed = jnp.dot(attended, w_output, preferred_element_type=jnp.float32).astype(jnp.bfloat16)
    return (mixed, new_entries)
```

```python
import jax
import jax.numpy as jnp
from jax import lax
from jax.sharding import PartitionSpec as P

FLOOR = -1e30


def rotate(values_in, positions):
    half_dim = values_in.shape[-1] // 2
    inverse_freq = 10000.0 ** (
        -(jnp.arange(half_dim, dtype=jnp.float32) * 2.0 / values_in.shape[-1])
    )
    angles = positions.astype(jnp.float32)[..., None] * inverse_freq
    angles = jnp.concatenate([angles, angles], -1)
    turned = jnp.concatenate([-values_in[..., half_dim:], values_in[..., :half_dim]], -1)
    return values_in * jnp.cos(angles) + turned * jnp.sin(angles)


def soft_part(scores, usable, value_rows, pattern):
    scores = jnp.where(usable, scores, FLOOR)
    peak = jnp.max(scores, -1)
    weights = jnp.where(usable, jnp.exp(scores - peak[..., None]), 0.0).astype(jnp.bfloat16)
    summed = jnp.einsum(pattern, weights, value_rows, preferred_element_type=jnp.float32)
    weight_sum = jnp.sum(weights.astype(jnp.float32), -1)
    return (summed, weight_sum, peak)


def split_two(values):
    high = values.astype(jnp.bfloat16)
    low = (values - high.astype(jnp.float32)).astype(jnp.bfloat16)
    return [high, low]


def split_three(values):
    high = values.astype(jnp.bfloat16)
    rest = values - high.astype(jnp.float32)
    middle = rest.astype(jnp.bfloat16)
    low = (rest - middle.astype(jnp.float32)).astype(jnp.bfloat16)
    return [high, middle, low]


def join(pieces):
    total = pieces[0].astype(jnp.float32)
    for piece in pieces[1:]:
        total = total + piece.astype(jnp.float32)
    return total


def local(
    hidden,
    norm_gain,
    w_query,
    w_keyval,
    w_output,
    node_cache,
    leaf_cache,
    leaf_branch,
    branch_root,
    root_owner,
    branch_owner,
    root_len,
    branch_len,
    leaf_len,
):
    head_dim = w_keyval.shape[1] // 2
    local_leaves = hidden.shape[0]
    group = w_query.shape[1] // head_dim
    factor = head_dim ** (-0.5)
    device = lax.axis_index("request")
    offset = device * local_leaves
    widened = hidden.astype(jnp.float32)
    normed = (
        widened * lax.rsqrt(jnp.mean(widened * widened, -1, keepdims=True) + 1e-05) * norm_gain
    ).astype(jnp.bfloat16)
    leaf_root = branch_root[leaf_branch]
    prefix_all = root_len[leaf_root] + branch_len[leaf_branch]
    positions = lax.dynamic_slice_in_dim(prefix_all, offset, local_leaves) + leaf_len
    raw_query = jnp.dot(normed, w_query, preferred_element_type=jnp.float32).reshape(
        local_leaves, group, head_dim
    )
    queries = rotate(raw_query, positions[:, None]).astype(jnp.bfloat16)
    everyone = lax.all_gather(
        queries.reshape(local_leaves, group * head_dim), "request", axis=0, tiled=True
    )
    raw_entry = jnp.dot(normed, w_keyval, preferred_element_type=jnp.float32)
    new_entry = jnp.concatenate(
        [rotate(raw_entry[:, :head_dim], positions), raw_entry[:, head_dim:]], -1
    ).astype(jnp.bfloat16)
    leaf_rows = leaf_cache[:, 0]
    slot_index = jnp.arange(leaf_rows.shape[1], dtype=jnp.int32)
    appended = jnp.where(
        (slot_index[None, :] == leaf_len[:, None])[:, :, None], new_entry[:, None, :], leaf_rows
    )
    leaf_scores = (
        jnp.einsum(
            "lgd,lkd->lgk", queries, appended[:, :, :head_dim], preferred_element_type=jnp.float32
        )
        * factor
    )
    leaf_usable = (slot_index[None, :] <= leaf_len[:, None])[:, None, :]
    leaf_sum, leaf_weight, leaf_peak = soft_part(
        leaf_scores, leaf_usable, appended[:, :, head_dim:], "lgk,lkd->lgd"
    )

    total_leaves = everyone.shape[0]
    root_mine = root_owner[leaf_root] == device
    branch_mine = branch_owner[leaf_branch] == device
    mine_all = root_mine | branch_mine
    my_length = jnp.sum(jnp.where(root_owner == device, root_len, 0)) + jnp.sum(
        jnp.where(branch_owner == device, branch_len, 0)
    )
    node_rows = node_cache[0, 0]
    node_usable = jnp.arange(node_rows.shape[0], dtype=jnp.int32) < my_length
    rows_query = everyone.reshape(total_leaves, group, head_dim)
    scores = (
        jnp.einsum(
            "ngd,kd->ngk", rows_query, node_rows[:, :head_dim], preferred_element_type=jnp.float32
        )
        * factor
    )
    usable = mine_all[:, None, None] & node_usable[None, None, :]
    own_sum, own_weight, own_peak = soft_part(scores, usable, node_rows[:, head_dim:], "ngk,kd->ngd")
    own_peak = jnp.where(mine_all[:, None], own_peak, 0.0)
    packet = jnp.concatenate(
        [own_sum.reshape(total_leaves, group * head_dim).astype(jnp.bfloat16)]
        + split_two(own_weight)
        + split_three(own_peak),
        -1,
    )
    zeros = jnp.zeros_like(packet)
    packet = jnp.stack(
        [
            jnp.where(root_mine[:, None], packet, zeros),
            jnp.where(branch_mine[:, None], packet, zeros),
        ],
        1,
    )
    width = packet.shape[-1]
    gathered = lax.psum_scatter(
        packet.reshape(total_leaves * 2, width), "request", scatter_dimension=0, tiled=True
    ).reshape(local_leaves, 2, width)
    sums = []
    weights = []
    peaks = []
    for part in range(2):
        piece = gathered[:, part]
        sums.append(
            piece[:, : group * head_dim].astype(jnp.float32).reshape(local_leaves, group, head_dim)
        )
        base = group * head_dim
        weights.append(join([piece[:, base + k * group : base + (k + 1) * group] for k in range(2)]))
        base = base + 2 * group
        peaks.append(join([piece[:, base + k * group : base + (k + 1) * group] for k in range(3)]))
    sums.append(leaf_sum)
    weights.append(leaf_weight)
    peaks.append(leaf_peak)
    peak = jnp.maximum(jnp.maximum(peaks[0], peaks[1]), peaks[2])
    numerator = jnp.zeros_like(leaf_sum)
    denominator = jnp.zeros_like(leaf_weight)
    for summed, weight_sum, part_peak in zip(sums, weights, peaks):
        scaled = jnp.exp(part_peak - peak)
        numerator = numerator + scaled[..., None] * summed
        denominator = denominator + scaled * weight_sum
    attended = (
        (numerator / denominator[..., None])
        .astype(jnp.bfloat16)
        .reshape(local_leaves, group * head_dim)
    )
    term = jnp.dot(attended, w_output, preferred_element_type=jnp.float32)
    mixed = lax.psum_scatter(term, "tensor", scatter_dimension=1, tiled=True).astype(jnp.bfloat16)
    return (mixed, new_entry[:, None, :])


def solution(mesh):
    in_specs = (
        P("request", None),
        P(),
        P(None, "tensor"),
        P(None, "tensor"),
        P("tensor", None),
        P("request", "tensor", None, None),
        P("request", "tensor", None, None),
        P(),
        P(),
        P(),
        P(),
        P(),
        P(),
        P("request"),
    )
    out_specs = (P("request", "tensor"), P("request", "tensor", None))
    return jax.shard_map(local, mesh=mesh, in_specs=in_specs, out_specs=out_specs, check_vma=False)
```

```python
import jax
import jax.numpy as jnp
from jax import lax
from jax.sharding import Mesh, PartitionSpec as P

FLOOR = -1e30


def rotate(values_in, positions):
    half_dim = values_in.shape[-1] // 2
    inverse_freq = 10000.0 ** (
        -(jnp.arange(half_dim, dtype=jnp.float32) * 2.0 / values_in.shape[-1])
    )
    angles = positions.astype(jnp.float32)[..., None] * inverse_freq
    angles = jnp.concatenate([angles, angles], -1)
    turned = jnp.concatenate([-values_in[..., half_dim:], values_in[..., :half_dim]], -1)
    return values_in * jnp.cos(angles) + turned * jnp.sin(angles)


def soft_part(scores, usable, value_rows, pattern):
    scores = jnp.where(usable, scores, FLOOR)
    peak = jnp.max(scores, -1)
    weights = jnp.where(usable, jnp.exp(scores - peak[..., None]), 0.0).astype(jnp.bfloat16)
    summed = jnp.einsum(pattern, weights, value_rows, preferred_element_type=jnp.float32)
    weight_sum = jnp.sum(weights.astype(jnp.float32), -1)
    return (summed, weight_sum, peak)


def split_two(values):
    high = values.astype(jnp.bfloat16)
    low = (values - high.astype(jnp.float32)).astype(jnp.bfloat16)
    return [high, low]


def split_three(values):
    high = values.astype(jnp.bfloat16)
    rest = values - high.astype(jnp.float32)
    middle = rest.astype(jnp.bfloat16)
    low = (rest - middle.astype(jnp.float32)).astype(jnp.bfloat16)
    return [high, middle, low]


def join(pieces):
    total = pieces[0].astype(jnp.float32)
    for piece in pieces[1:]:
        total = total + piece.astype(jnp.float32)
    return total


def local(
    hidden,
    norm_gain,
    w_query,
    w_keyval,
    w_output,
    node_cache,
    leaf_cache,
    leaf_branch,
    branch_root,
    root_owner,
    branch_owner,
    root_len,
    branch_len,
    leaf_len,
):
    head_dim = w_keyval.shape[1] // 2
    local_leaves = hidden.shape[0]
    group = w_query.shape[1] // head_dim
    factor = head_dim ** (-0.5)
    device = (
        lax.axis_index("z") * (lax.axis_size("y") * lax.axis_size("core"))
        + lax.axis_index("y") * lax.axis_size("core")
        + lax.axis_index("core")
    )
    offset = device * local_leaves
    widened = hidden.astype(jnp.float32)
    normed = (
        widened * lax.rsqrt(jnp.mean(widened * widened, -1, keepdims=True) + 1e-05) * norm_gain
    ).astype(jnp.bfloat16)
    branch_ids = jnp.arange(branch_root.shape[0], dtype=jnp.int32)
    root_ids = jnp.arange(root_owner.shape[0], dtype=jnp.int32)
    own_branch = lax.dynamic_slice_in_dim(leaf_branch, offset, local_leaves)
    own_hits = own_branch[:, None] == branch_ids[None, :]
    own_root = jnp.sum(jnp.where(own_hits, branch_root[None, :], 0), 1)
    positions = (
        jnp.sum(jnp.where(own_root[:, None] == root_ids[None, :], root_len[None, :], 0), 1)
        + jnp.sum(jnp.where(own_hits, branch_len[None, :], 0), 1)
        + leaf_len
    )
    raw_query = jnp.dot(normed, w_query, preferred_element_type=jnp.float32).reshape(
        local_leaves, group, head_dim
    )
    queries = rotate(raw_query, positions[:, None]).astype(jnp.bfloat16)
    everyone = lax.all_gather(
        lax.all_gather(
            queries.reshape(local_leaves, group * head_dim), "z", axis=0, tiled=True
        ),
        ("y", "core"),
        axis=0,
        tiled=True,
    )
    raw_entry = jnp.dot(normed, w_keyval, preferred_element_type=jnp.float32)
    new_entry = jnp.concatenate(
        [rotate(raw_entry[:, :head_dim], positions), raw_entry[:, head_dim:]], -1
    ).astype(jnp.bfloat16)
    leaf_rows = leaf_cache[:, 0]
    slot_index = jnp.arange(leaf_rows.shape[1], dtype=jnp.int32)
    appended = jnp.where(
        (slot_index[None, :] == leaf_len[:, None])[:, :, None], new_entry[:, None, :], leaf_rows
    )
    leaf_scores = (
        jnp.einsum(
            "lgd,lkd->lgk", queries, appended[:, :, :head_dim], preferred_element_type=jnp.float32
        )
        * factor
    )
    leaf_usable = (slot_index[None, :] <= leaf_len[:, None])[:, None, :]
    leaf_sum, leaf_weight, leaf_peak = soft_part(
        leaf_scores, leaf_usable, appended[:, :, head_dim:], "lgk,lkd->lgd"
    )

    total_leaves = everyone.shape[0]
    z_size = lax.axis_size("z")
    row_branch = (
        leaf_branch.reshape(z_size, total_leaves // (z_size * local_leaves), local_leaves)
        .transpose(1, 0, 2)
        .reshape(total_leaves)
    )
    branch_root_hits = branch_root[:, None] == root_ids[None, :]
    root_mine_by_branch = jnp.any(branch_root_hits & (root_owner == device)[None, :], 1)
    row_hits = row_branch[:, None] == branch_ids[None, :]
    root_mine = jnp.any(row_hits & root_mine_by_branch[None, :], 1)
    branch_mine = jnp.any(row_hits & (branch_owner == device)[None, :], 1)
    mine_all = root_mine | branch_mine
    my_length = jnp.sum(jnp.where(root_owner == device, root_len, 0)) + jnp.sum(
        jnp.where(branch_owner == device, branch_len, 0)
    )
    node_rows = node_cache[0, 0]
    node_usable = jnp.arange(node_rows.shape[0], dtype=jnp.int32) < my_length
    rows_query = everyone.reshape(total_leaves, group, head_dim)
    scores = (
        jnp.einsum(
            "ngd,kd->ngk", rows_query, node_rows[:, :head_dim], preferred_element_type=jnp.float32
        )
        * factor
    )
    usable = mine_all[:, None, None] & node_usable[None, None, :]
    own_sum, own_weight, own_peak = soft_part(scores, usable, node_rows[:, head_dim:], "ngk,kd->ngd")
    own_peak = jnp.where(mine_all[:, None], own_peak, 0.0)
    packet = jnp.concatenate(
        [own_sum.reshape(total_leaves, group * head_dim).astype(jnp.bfloat16)]
        + split_two(own_weight)
        + split_three(own_peak),
        -1,
    )
    zeros = jnp.zeros_like(packet)
    packet = jnp.stack(
        [
            jnp.where(root_mine[:, None], packet, zeros),
            jnp.where(branch_mine[:, None], packet, zeros),
        ],
        1,
    )
    width = packet.shape[-1]
    gathered = lax.psum_scatter(
        lax.psum_scatter(
            packet.reshape(total_leaves * 2, width), ("y", "core"), scatter_dimension=0, tiled=True
        ),
        "z",
        scatter_dimension=0,
        tiled=True,
    ).reshape(local_leaves, 2, width)
    sums = []
    weights = []
    peaks = []
    for part in range(2):
        piece = gathered[:, part]
        sums.append(
            piece[:, : group * head_dim].astype(jnp.float32).reshape(local_leaves, group, head_dim)
        )
        base = group * head_dim
        weights.append(join([piece[:, base + k * group : base + (k + 1) * group] for k in range(2)]))
        base = base + 2 * group
        peaks.append(join([piece[:, base + k * group : base + (k + 1) * group] for k in range(3)]))
    sums.append(leaf_sum)
    weights.append(leaf_weight)
    peaks.append(leaf_peak)
    peak = jnp.maximum(jnp.maximum(peaks[0], peaks[1]), peaks[2])
    numerator = jnp.zeros_like(leaf_sum)
    denominator = jnp.zeros_like(leaf_weight)
    for summed, weight_sum, part_peak in zip(sums, weights, peaks):
        scaled = jnp.exp(part_peak - peak)
        numerator = numerator + scaled[..., None] * summed
        denominator = denominator + scaled * weight_sum
    attended = (
        (numerator / denominator[..., None])
        .astype(jnp.bfloat16)
        .reshape(local_leaves, group * head_dim)
    )
    term = jnp.dot(attended, w_output, preferred_element_type=jnp.float32)
    mixed = lax.psum_scatter(term, "tensor", scatter_dimension=1, tiled=True).astype(jnp.bfloat16)
    return (mixed, new_entry[:, None, :])


def solution(mesh):
    tensor_size = mesh.shape["tensor"]
    request_size = mesh.shape["request"]
    core_size = 2
    y_size = 4
    z_size = request_size // (y_size * core_size)
    fine = Mesh(
        mesh.devices.reshape(tensor_size, z_size, y_size, core_size),
        ("tensor", "z", "y", "core"),
    )
    request = ("z", "y", "core")
    in_specs = (
        P(request, None),
        P(),
        P(None, "tensor"),
        P(None, "tensor"),
        P("tensor", None),
        P(request, "tensor", None, None),
        P(request, "tensor", None, None),
        P(),
        P(),
        P(),
        P(),
        P(),
        P(),
        P(request),
    )
    out_specs = (P(request, "tensor"), P(request, "tensor", None))
    return jax.shard_map(local, mesh=fine, in_specs=in_specs, out_specs=out_specs, check_vma=False)
```

```python
import jax
import jax.numpy as jnp
from jax import lax
from jax.sharding import Mesh, PartitionSpec as P

FLOOR = -1e30


def rotate(values_in, positions):
    half_dim = values_in.shape[-1] // 2
    inverse_freq = 10000.0 ** (
        -(jnp.arange(half_dim, dtype=jnp.float32) * 2.0 / values_in.shape[-1])
    )
    angles = positions.astype(jnp.float32)[..., None] * inverse_freq
    angles = jnp.concatenate([angles, angles], -1)
    turned = jnp.concatenate([-values_in[..., half_dim:], values_in[..., :half_dim]], -1)
    return values_in * jnp.cos(angles) + turned * jnp.sin(angles)


def soft_part(scores, usable, value_rows, pattern):
    scores = jnp.where(usable, scores, FLOOR)
    peak = jnp.max(scores, -1)
    weights = jnp.where(usable, jnp.exp(scores - peak[..., None]), 0.0).astype(jnp.bfloat16)
    summed = jnp.einsum(pattern, weights, value_rows, preferred_element_type=jnp.float32)
    weight_sum = jnp.sum(weights.astype(jnp.float32), -1)
    return (summed, weight_sum, peak)


def split_two(values):
    high = values.astype(jnp.bfloat16)
    low = (values - high.astype(jnp.float32)).astype(jnp.bfloat16)
    return [high, low]


def split_three(values):
    high = values.astype(jnp.bfloat16)
    rest = values - high.astype(jnp.float32)
    middle = rest.astype(jnp.bfloat16)
    low = (rest - middle.astype(jnp.float32)).astype(jnp.bfloat16)
    return [high, middle, low]


def join(pieces):
    total = pieces[0].astype(jnp.float32)
    for piece in pieces[1:]:
        total = total + piece.astype(jnp.float32)
    return total


def group_size(axes):
    size = 1
    for axis in axes if isinstance(axes, tuple) else (axes,):
        size = size * lax.axis_size(axis)
    return size


def gather_rows(values, axes):
    count = group_size(axes)
    spread = jnp.broadcast_to(values[None], (count,) + values.shape)
    received = lax.all_to_all(spread, axes, 0, 0, tiled=False)
    return received.reshape(count * values.shape[0], values.shape[1])


def scatter_rows(values, axes):
    count = group_size(axes)
    blocks = values.reshape(count, values.shape[0] // count, values.shape[1])
    received = lax.all_to_all(blocks, axes, 0, 0, tiled=False)
    return jnp.sum(received.astype(jnp.float32), 0).astype(values.dtype)


def local(
    hidden,
    norm_gain,
    w_query,
    w_keyval,
    w_output,
    node_cache,
    leaf_cache,
    leaf_branch,
    branch_root,
    root_owner,
    branch_owner,
    root_len,
    branch_len,
    leaf_len,
):
    head_dim = w_keyval.shape[1] // 2
    local_leaves = hidden.shape[0]
    group = w_query.shape[1] // head_dim
    factor = head_dim ** (-0.5)
    device = (
        lax.axis_index("z") * (lax.axis_size("y") * lax.axis_size("core"))
        + lax.axis_index("y") * lax.axis_size("core")
        + lax.axis_index("core")
    )
    offset = device * local_leaves
    widened = hidden.astype(jnp.float32)
    normed = (
        widened * lax.rsqrt(jnp.mean(widened * widened, -1, keepdims=True) + 1e-05) * norm_gain
    ).astype(jnp.bfloat16)
    branch_ids = jnp.arange(branch_root.shape[0], dtype=jnp.int32)
    root_ids = jnp.arange(root_owner.shape[0], dtype=jnp.int32)
    own_branch = lax.dynamic_slice_in_dim(leaf_branch, offset, local_leaves)
    own_hits = own_branch[:, None] == branch_ids[None, :]
    own_root = jnp.sum(jnp.where(own_hits, branch_root[None, :], 0), 1)
    positions = (
        jnp.sum(jnp.where(own_root[:, None] == root_ids[None, :], root_len[None, :], 0), 1)
        + jnp.sum(jnp.where(own_hits, branch_len[None, :], 0), 1)
        + leaf_len
    )
    raw_query = jnp.dot(normed, w_query, preferred_element_type=jnp.float32).reshape(
        local_leaves, group, head_dim
    )
    queries = rotate(raw_query, positions[:, None]).astype(jnp.bfloat16)
    everyone = gather_rows(
        gather_rows(queries.reshape(local_leaves, group * head_dim), "z"), ("y", "core")
    )
    raw_entry = jnp.dot(normed, w_keyval, preferred_element_type=jnp.float32)
    new_entry = jnp.concatenate(
        [rotate(raw_entry[:, :head_dim], positions), raw_entry[:, head_dim:]], -1
    ).astype(jnp.bfloat16)
    leaf_rows = leaf_cache[:, 0]
    slot_index = jnp.arange(leaf_rows.shape[1], dtype=jnp.int32)
    appended = jnp.where(
        (slot_index[None, :] == leaf_len[:, None])[:, :, None], new_entry[:, None, :], leaf_rows
    )
    leaf_scores = (
        jnp.einsum(
            "lgd,lkd->lgk", queries, appended[:, :, :head_dim], preferred_element_type=jnp.float32
        )
        * factor
    )
    leaf_usable = (slot_index[None, :] <= leaf_len[:, None])[:, None, :]
    leaf_sum, leaf_weight, leaf_peak = soft_part(
        leaf_scores, leaf_usable, appended[:, :, head_dim:], "lgk,lkd->lgd"
    )

    total_leaves = everyone.shape[0]
    z_size = lax.axis_size("z")
    row_branch = (
        leaf_branch.reshape(z_size, total_leaves // (z_size * local_leaves), local_leaves)
        .transpose(1, 0, 2)
        .reshape(total_leaves)
    )
    branch_root_hits = branch_root[:, None] == root_ids[None, :]
    root_mine_by_branch = jnp.any(branch_root_hits & (root_owner == device)[None, :], 1)
    row_hits = row_branch[:, None] == branch_ids[None, :]
    root_mine = jnp.any(row_hits & root_mine_by_branch[None, :], 1)
    branch_mine = jnp.any(row_hits & (branch_owner == device)[None, :], 1)
    mine_all = root_mine | branch_mine
    my_length = jnp.sum(jnp.where(root_owner == device, root_len, 0)) + jnp.sum(
        jnp.where(branch_owner == device, branch_len, 0)
    )
    node_rows = node_cache[0, 0]
    node_usable = jnp.arange(node_rows.shape[0], dtype=jnp.int32) < my_length
    rows_query = everyone.reshape(total_leaves, group, head_dim)
    scores = (
        jnp.einsum(
            "ngd,kd->ngk", rows_query, node_rows[:, :head_dim], preferred_element_type=jnp.float32
        )
        * factor
    )
    usable = mine_all[:, None, None] & node_usable[None, None, :]
    own_sum, own_weight, own_peak = soft_part(scores, usable, node_rows[:, head_dim:], "ngk,kd->ngd")
    own_peak = jnp.where(mine_all[:, None], own_peak, 0.0)
    packet = jnp.concatenate(
        [own_sum.reshape(total_leaves, group * head_dim).astype(jnp.bfloat16)]
        + split_two(own_weight)
        + split_three(own_peak),
        -1,
    )
    zeros = jnp.zeros_like(packet)
    packet = jnp.stack(
        [
            jnp.where(root_mine[:, None], packet, zeros),
            jnp.where(branch_mine[:, None], packet, zeros),
        ],
        1,
    )
    width = packet.shape[-1]
    gathered = scatter_rows(
        scatter_rows(packet.reshape(total_leaves * 2, width), ("y", "core")), "z"
    ).reshape(local_leaves, 2, width)
    sums = []
    weights = []
    peaks = []
    for part in range(2):
        piece = gathered[:, part]
        sums.append(
            piece[:, : group * head_dim].astype(jnp.float32).reshape(local_leaves, group, head_dim)
        )
        base = group * head_dim
        weights.append(join([piece[:, base + k * group : base + (k + 1) * group] for k in range(2)]))
        base = base + 2 * group
        peaks.append(join([piece[:, base + k * group : base + (k + 1) * group] for k in range(3)]))
    sums.append(leaf_sum)
    weights.append(leaf_weight)
    peaks.append(leaf_peak)
    peak = jnp.maximum(jnp.maximum(peaks[0], peaks[1]), peaks[2])
    numerator = jnp.zeros_like(leaf_sum)
    denominator = jnp.zeros_like(leaf_weight)
    for summed, weight_sum, part_peak in zip(sums, weights, peaks):
        scaled = jnp.exp(part_peak - peak)
        numerator = numerator + scaled[..., None] * summed
        denominator = denominator + scaled * weight_sum
    attended = (
        (numerator / denominator[..., None])
        .astype(jnp.bfloat16)
        .reshape(local_leaves, group * head_dim)
    )
    term = jnp.dot(attended, w_output, preferred_element_type=jnp.float32)
    tensor_size = lax.axis_size("tensor")
    pieces = lax.all_to_all(
        term.reshape(local_leaves, tensor_size, term.shape[1] // tensor_size),
        "tensor",
        1,
        1,
        tiled=False,
    )
    mixed = jnp.sum(pieces, 1).astype(jnp.bfloat16)
    return (mixed, new_entry[:, None, :])


def solution(mesh):
    tensor_size = mesh.shape["tensor"]
    request_size = mesh.shape["request"]
    core_size = 2
    y_size = 4
    z_size = request_size // (y_size * core_size)
    fine = Mesh(
        mesh.devices.reshape(tensor_size, z_size, y_size, core_size),
        ("tensor", "z", "y", "core"),
    )
    request = ("z", "y", "core")
    in_specs = (
        P(request, None),
        P(),
        P(None, "tensor"),
        P(None, "tensor"),
        P("tensor", None),
        P(request, "tensor", None, None),
        P(request, "tensor", None, None),
        P(),
        P(),
        P(),
        P(),
        P(),
        P(),
        P(request),
    )
    out_specs = (P(request, "tensor"), P(request, "tensor", None))
    return jax.shard_map(local, mesh=fine, in_specs=in_specs, out_specs=out_specs, check_vma=False)
```

```python
import jax
import jax.numpy as jnp
from jax import lax
from jax.sharding import Mesh, PartitionSpec as P

FLOOR = -1e30


def rotate(values_in, positions):
    half_dim = values_in.shape[-1] // 2
    inverse_freq = 10000.0 ** (
        -(jnp.arange(half_dim, dtype=jnp.float32) * 2.0 / values_in.shape[-1])
    )
    angles = positions.astype(jnp.float32)[..., None] * inverse_freq
    angles = jnp.concatenate([angles, angles], -1)
    turned = jnp.concatenate([-values_in[..., half_dim:], values_in[..., :half_dim]], -1)
    return values_in * jnp.cos(angles) + turned * jnp.sin(angles)


def soft_part(scores, usable, value_rows, pattern):
    scores = jnp.where(usable, scores, FLOOR)
    peak = jnp.max(scores, -1)
    weights = jnp.where(usable, jnp.exp(scores - peak[..., None]), 0.0).astype(jnp.bfloat16)
    summed = jnp.einsum(pattern, weights, value_rows, preferred_element_type=jnp.float32)
    weight_sum = jnp.sum(weights.astype(jnp.float32), -1)
    return (summed, weight_sum, peak)


def split_two(values):
    high = values.astype(jnp.bfloat16)
    low = (values - high.astype(jnp.float32)).astype(jnp.bfloat16)
    return [high, low]


def split_three(values):
    high = values.astype(jnp.bfloat16)
    rest = values - high.astype(jnp.float32)
    middle = rest.astype(jnp.bfloat16)
    low = (rest - middle.astype(jnp.float32)).astype(jnp.bfloat16)
    return [high, middle, low]


def join(pieces):
    total = pieces[0].astype(jnp.float32)
    for piece in pieces[1:]:
        total = total + piece.astype(jnp.float32)
    return total


def group_size(axes):
    size = 1
    for axis in axes if isinstance(axes, tuple) else (axes,):
        size = size * lax.axis_size(axis)
    return size


def gather_rows(values, axes):
    count = group_size(axes)
    spread = jnp.broadcast_to(values[None], (count,) + values.shape)
    received = lax.all_to_all(spread, axes, 0, 0, tiled=False)
    return received.reshape(count * values.shape[0], values.shape[1])


def scatter_rows(values, axes):
    count = group_size(axes)
    blocks = values.reshape(count, values.shape[0] // count, values.shape[1])
    received = lax.all_to_all(blocks, axes, 0, 0, tiled=False)
    return jnp.sum(received.astype(jnp.float32), 0).astype(values.dtype)


def local(
    hidden,
    norm_gain,
    w_query,
    w_keyval,
    w_output,
    node_cache,
    leaf_cache,
    leaf_branch,
    branch_root,
    root_owner,
    branch_owner,
    root_len,
    branch_len,
    leaf_len,
):
    head_dim = w_keyval.shape[1] // 2
    local_leaves = hidden.shape[0]
    group = w_query.shape[1] // head_dim
    factor = head_dim ** (-0.5)
    device = (
        lax.axis_index("z") * (lax.axis_size("y") * lax.axis_size("core"))
        + lax.axis_index("y") * lax.axis_size("core")
        + lax.axis_index("core")
    )
    offset = device * local_leaves
    widened = hidden.astype(jnp.float32)
    normed = (
        widened * lax.rsqrt(jnp.mean(widened * widened, -1, keepdims=True) + 1e-05) * norm_gain
    ).astype(jnp.bfloat16)
    branch_ids = jnp.arange(branch_root.shape[0], dtype=jnp.int32)
    root_ids = jnp.arange(root_owner.shape[0], dtype=jnp.int32)
    own_branch = lax.dynamic_slice_in_dim(leaf_branch, offset, local_leaves)
    own_hits = own_branch[:, None] == branch_ids[None, :]
    own_root = jnp.sum(jnp.where(own_hits, branch_root[None, :], 0), 1)
    positions = (
        jnp.sum(jnp.where(own_root[:, None] == root_ids[None, :], root_len[None, :], 0), 1)
        + jnp.sum(jnp.where(own_hits, branch_len[None, :], 0), 1)
        + leaf_len
    )
    raw_query = jnp.dot(normed, w_query, preferred_element_type=jnp.float32).reshape(
        local_leaves, group, head_dim
    )
    queries = rotate(raw_query, positions[:, None]).astype(jnp.bfloat16)
    everyone = gather_rows(
        gather_rows(queries.reshape(local_leaves, group * head_dim), "z"), ("y", "core")
    )
    raw_entry = jnp.dot(normed, w_keyval, preferred_element_type=jnp.float32)
    new_entry = jnp.concatenate(
        [rotate(raw_entry[:, :head_dim], positions), raw_entry[:, head_dim:]], -1
    ).astype(jnp.bfloat16)
    leaf_rows = leaf_cache[:, 0]
    slot_index = jnp.arange(leaf_rows.shape[1], dtype=jnp.int32)
    appended = jnp.where(
        (slot_index[None, :] == leaf_len[:, None])[:, :, None], new_entry[:, None, :], leaf_rows
    )
    leaf_scores = (
        jnp.einsum(
            "lgd,lkd->lgk", queries, appended[:, :, :head_dim], preferred_element_type=jnp.float32
        )
        * factor
    )
    leaf_usable = (slot_index[None, :] <= leaf_len[:, None])[:, None, :]
    leaf_sum, leaf_weight, leaf_peak = soft_part(
        leaf_scores, leaf_usable, appended[:, :, head_dim:], "lgk,lkd->lgd"
    )

    total_leaves = everyone.shape[0]
    z_size = lax.axis_size("z")
    row_branch = (
        leaf_branch.reshape(z_size, total_leaves // (z_size * local_leaves), local_leaves)
        .transpose(1, 0, 2)
        .reshape(total_leaves)
    )
    branch_root_hits = branch_root[:, None] == root_ids[None, :]
    root_mine_by_branch = jnp.any(branch_root_hits & (root_owner == device)[None, :], 1)
    row_hits = row_branch[:, None] == branch_ids[None, :]
    root_mine = jnp.any(row_hits & root_mine_by_branch[None, :], 1)
    branch_mine = jnp.any(row_hits & (branch_owner == device)[None, :], 1)
    mine_all = root_mine | branch_mine
    my_length = jnp.sum(jnp.where(root_owner == device, root_len, 0)) + jnp.sum(
        jnp.where(branch_owner == device, branch_len, 0)
    )
    node_rows = node_cache[0, 0]
    node_usable = jnp.arange(node_rows.shape[0], dtype=jnp.int32) < my_length
    rows_query = everyone.reshape(total_leaves, group, head_dim)
    scores = (
        jnp.einsum(
            "ngd,kd->ngk", rows_query, node_rows[:, :head_dim], preferred_element_type=jnp.float32
        )
        * factor
    )
    usable = mine_all[:, None, None] & node_usable[None, None, :]
    own_sum, own_weight, own_peak = soft_part(scores, usable, node_rows[:, head_dim:], "ngk,kd->ngd")
    own_peak = jnp.where(mine_all[:, None], own_peak, 0.0)
    own_values = own_sum.reshape(total_leaves, group * head_dim).astype(jnp.bfloat16)
    own_stats = jnp.concatenate(split_two(own_weight) + split_three(own_peak), -1)
    stat_width = own_stats.shape[1]
    pad_width = (-(2 * group * head_dim + 2 * stat_width)) % 128
    zeros_values = jnp.zeros_like(own_values)
    zeros_stats = jnp.zeros_like(own_stats)
    packet = jnp.concatenate(
        [
            jnp.where(root_mine[:, None], own_values, zeros_values),
            jnp.where(branch_mine[:, None], own_values, zeros_values),
            jnp.where(root_mine[:, None], own_stats, zeros_stats),
            jnp.where(branch_mine[:, None], own_stats, zeros_stats),
            jnp.zeros((total_leaves, pad_width), jnp.bfloat16),
        ],
        -1,
    )
    gathered = scatter_rows(scatter_rows(packet, ("y", "core")), "z")
    sums = []
    weights = []
    peaks = []
    for part in range(2):
        sums.append(
            gathered[:, part * group * head_dim : (part + 1) * group * head_dim]
            .astype(jnp.float32)
            .reshape(local_leaves, group, head_dim)
        )
        base = 2 * group * head_dim + part * stat_width
        weights.append(join([gathered[:, base + k * group : base + (k + 1) * group] for k in range(2)]))
        base = base + 2 * group
        peaks.append(join([gathered[:, base + k * group : base + (k + 1) * group] for k in range(3)]))
    sums.append(leaf_sum)
    weights.append(leaf_weight)
    peaks.append(leaf_peak)
    peak = jnp.maximum(jnp.maximum(peaks[0], peaks[1]), peaks[2])
    numerator = jnp.zeros_like(leaf_sum)
    denominator = jnp.zeros_like(leaf_weight)
    for summed, weight_sum, part_peak in zip(sums, weights, peaks):
        scaled = jnp.exp(part_peak - peak)
        numerator = numerator + scaled[..., None] * summed
        denominator = denominator + scaled * weight_sum
    attended = (
        (numerator / denominator[..., None])
        .astype(jnp.bfloat16)
        .reshape(local_leaves, group * head_dim)
    )
    term = jnp.dot(attended, w_output, preferred_element_type=jnp.float32)
    tensor_size = lax.axis_size("tensor")
    pieces = lax.all_to_all(
        term.reshape(local_leaves, tensor_size, term.shape[1] // tensor_size),
        "tensor",
        1,
        1,
        tiled=False,
    )
    mixed = jnp.sum(pieces, 1).astype(jnp.bfloat16)
    return (mixed, new_entry[:, None, :])


def solution(mesh):
    tensor_size = mesh.shape["tensor"]
    request_size = mesh.shape["request"]
    core_size = 2
    y_size = 4
    z_size = request_size // (y_size * core_size)
    fine = Mesh(
        mesh.devices.reshape(tensor_size, z_size, y_size, core_size),
        ("tensor", "z", "y", "core"),
    )
    request = ("z", "y", "core")
    in_specs = (
        P(request, None),
        P(),
        P(None, "tensor"),
        P(None, "tensor"),
        P("tensor", None),
        P(request, "tensor", None, None),
        P(request, "tensor", None, None),
        P(),
        P(),
        P(),
        P(),
        P(),
        P(),
        P(request),
    )
    out_specs = (P(request, "tensor"), P(request, "tensor", None))
    return jax.shard_map(local, mesh=fine, in_specs=in_specs, out_specs=out_specs, check_vma=False)
```

```python
import jax
import jax.numpy as jnp
from jax import lax
from jax.sharding import Mesh, PartitionSpec as P

FLOOR = -1e30


def rotate(values_in, positions):
    half_dim = values_in.shape[-1] // 2
    inverse_freq = 10000.0 ** (
        -(jnp.arange(half_dim, dtype=jnp.float32) * 2.0 / values_in.shape[-1])
    )
    angles = positions.astype(jnp.float32)[..., None] * inverse_freq
    angles = jnp.concatenate([angles, angles], -1)
    turned = jnp.concatenate([-values_in[..., half_dim:], values_in[..., :half_dim]], -1)
    return values_in * jnp.cos(angles) + turned * jnp.sin(angles)


def soft_part(scores, usable, value_rows, pattern):
    scores = jnp.where(usable, scores, FLOOR)
    peak = jnp.max(scores, -1)
    weights = jnp.where(usable, jnp.exp(scores - peak[..., None]), 0.0).astype(jnp.bfloat16)
    summed = jnp.einsum(pattern, weights, value_rows, preferred_element_type=jnp.float32)
    weight_sum = jnp.sum(weights.astype(jnp.float32), -1)
    return (summed, weight_sum, peak)


def split_two(values):
    high = values.astype(jnp.bfloat16)
    low = (values - high.astype(jnp.float32)).astype(jnp.bfloat16)
    return [high, low]


def split_three(values):
    high = values.astype(jnp.bfloat16)
    rest = values - high.astype(jnp.float32)
    middle = rest.astype(jnp.bfloat16)
    low = (rest - middle.astype(jnp.float32)).astype(jnp.bfloat16)
    return [high, middle, low]


def join(pieces):
    total = pieces[0].astype(jnp.float32)
    for piece in pieces[1:]:
        total = total + piece.astype(jnp.float32)
    return total


def group_size(axes):
    size = 1
    for axis in axes if isinstance(axes, tuple) else (axes,):
        size = size * lax.axis_size(axis)
    return size


def gather_rows(values, axes):
    count = group_size(axes)
    spread = jnp.broadcast_to(values[None], (count,) + values.shape)
    received = lax.all_to_all(spread, axes, 0, 0, tiled=False)
    return received.reshape(count * values.shape[0], values.shape[1])


def scatter_rows(values, axes):
    count = group_size(axes)
    blocks = values.reshape(count, values.shape[0] // count, values.shape[1])
    received = lax.all_to_all(blocks, axes, 0, 0, tiled=False)
    return jnp.sum(received.astype(jnp.float32), 0).astype(values.dtype)


def local(
    hidden,
    norm_gain,
    w_query,
    w_keyval,
    w_output,
    node_cache,
    leaf_cache,
    leaf_branch,
    branch_root,
    root_owner,
    branch_owner,
    root_len,
    branch_len,
    leaf_len,
):
    head_dim = w_keyval.shape[1] // 2
    local_leaves = hidden.shape[0]
    group = w_query.shape[1] // head_dim
    factor = head_dim ** (-0.5)
    device = (
        lax.axis_index("z") * (lax.axis_size("y") * lax.axis_size("core"))
        + lax.axis_index("y") * lax.axis_size("core")
        + lax.axis_index("core")
    )
    offset = device * local_leaves
    widened = hidden.astype(jnp.float32)
    normed = (
        widened * lax.rsqrt(jnp.mean(widened * widened, -1, keepdims=True) + 1e-05) * norm_gain
    ).astype(jnp.bfloat16)
    branch_ids = jnp.arange(branch_root.shape[0], dtype=jnp.int32)
    root_ids = jnp.arange(root_owner.shape[0], dtype=jnp.int32)
    own_branch = lax.dynamic_slice_in_dim(leaf_branch, offset, local_leaves)
    own_hits = own_branch[:, None] == branch_ids[None, :]
    own_root = jnp.sum(jnp.where(own_hits, branch_root[None, :], 0), 1)
    positions = (
        jnp.sum(jnp.where(own_root[:, None] == root_ids[None, :], root_len[None, :], 0), 1)
        + jnp.sum(jnp.where(own_hits, branch_len[None, :], 0), 1)
        + leaf_len
    )
    raw_query = jnp.dot(normed, w_query, preferred_element_type=jnp.float32).reshape(
        local_leaves, group, head_dim
    )
    queries = rotate(raw_query, positions[:, None]).astype(jnp.bfloat16)
    everyone = gather_rows(queries.reshape(local_leaves, group * head_dim), "z")
    node_rows = node_cache[0, 0]
    slots = gather_rows(node_rows, ("y", "core")).reshape(
        -1, node_rows.shape[0], node_rows.shape[1]
    )
    raw_entry = jnp.dot(normed, w_keyval, preferred_element_type=jnp.float32)
    new_entry = jnp.concatenate(
        [rotate(raw_entry[:, :head_dim], positions), raw_entry[:, head_dim:]], -1
    ).astype(jnp.bfloat16)
    leaf_rows = leaf_cache[:, 0]
    slot_index = jnp.arange(leaf_rows.shape[1], dtype=jnp.int32)
    appended = jnp.where(
        (slot_index[None, :] == leaf_len[:, None])[:, :, None], new_entry[:, None, :], leaf_rows
    )
    leaf_scores = (
        jnp.einsum(
            "lgd,lkd->lgk", queries, appended[:, :, :head_dim], preferred_element_type=jnp.float32
        )
        * factor
    )
    leaf_usable = (slot_index[None, :] <= leaf_len[:, None])[:, None, :]
    leaf_sum, leaf_weight, leaf_peak = soft_part(
        leaf_scores, leaf_usable, appended[:, :, head_dim:], "lgk,lkd->lgd"
    )

    row_count = everyone.shape[0]
    slot_count = slots.shape[0]
    z_size = lax.axis_size("z")
    my_y_core = device % slot_count
    first_slot = device - my_y_core
    row_branch = lax.dynamic_slice_in_dim(
        leaf_branch.reshape(z_size, slot_count * local_leaves),
        my_y_core * local_leaves,
        local_leaves,
        axis=1,
    ).reshape(row_count)
    slot_ids = first_slot + jnp.arange(slot_count, dtype=jnp.int32)
    branch_root_hits = branch_root[:, None] == root_ids[None, :]
    root_slot_of_branch = jnp.any(
        branch_root_hits[:, None, :] & (root_owner[None, None, :] == slot_ids[None, :, None]), 2
    )
    branch_slot_of_branch = branch_owner[:, None] == slot_ids[None, :]
    row_hits = row_branch[:, None] == branch_ids[None, :]
    root_mine = jnp.any(row_hits[:, :, None] & root_slot_of_branch[None, :, :], 1)
    branch_mine = jnp.any(row_hits[:, :, None] & branch_slot_of_branch[None, :, :], 1)
    mine_all = root_mine | branch_mine
    slot_length = jnp.sum(
        jnp.where(root_owner[None, :] == slot_ids[:, None], root_len[None, :], 0), 1
    ) + jnp.sum(jnp.where(branch_owner[None, :] == slot_ids[:, None], branch_len[None, :], 0), 1)
    node_usable = (
        jnp.arange(slots.shape[1], dtype=jnp.int32)[None, :] < slot_length[:, None]
    )
    rows_query = everyone.reshape(row_count, group, head_dim)
    scores = (
        jnp.einsum(
            "ngd,skd->nsgk", rows_query, slots[:, :, :head_dim], preferred_element_type=jnp.float32
        )
        * factor
    )
    usable = mine_all[:, :, None, None] & node_usable[None, :, None, :]
    slot_sum, slot_weight, slot_peak = soft_part(
        scores, usable, slots[:, :, head_dim:], "nsgk,skd->nsgd"
    )
    slot_peak = jnp.where(mine_all[:, :, None], slot_peak, 0.0)

    def pick(mask, values):
        shape = mask.shape + (1,) * (values.ndim - mask.ndim)
        return jnp.sum(jnp.where(mask.reshape(shape), values, 0.0), 1)

    parts = [
        (pick(mask, slot_sum), pick(mask, slot_weight), pick(mask, slot_peak))
        for mask in (root_mine, branch_mine)
    ]
    pieces = []
    stats = []
    for part_sum, part_weight, part_peak in parts:
        pieces.append(part_sum.reshape(row_count, group * head_dim).astype(jnp.bfloat16))
        stats.append(jnp.concatenate(split_two(part_weight) + split_three(part_peak), -1))
    stat_width = stats[0].shape[1]
    pad_width = (-(2 * group * head_dim + 2 * stat_width)) % 128
    packet = jnp.concatenate(
        pieces + stats + [jnp.zeros((row_count, pad_width), jnp.bfloat16)], -1
    )
    gathered = scatter_rows(packet, "z")
    sums = []
    weights = []
    peaks = []
    for part in range(2):
        sums.append(
            gathered[:, part * group * head_dim : (part + 1) * group * head_dim]
            .astype(jnp.float32)
            .reshape(local_leaves, group, head_dim)
        )
        base = 2 * group * head_dim + part * stat_width
        weights.append(join([gathered[:, base + k * group : base + (k + 1) * group] for k in range(2)]))
        base = base + 2 * group
        peaks.append(join([gathered[:, base + k * group : base + (k + 1) * group] for k in range(3)]))
    sums.append(leaf_sum)
    weights.append(leaf_weight)
    peaks.append(leaf_peak)
    peak = jnp.maximum(jnp.maximum(peaks[0], peaks[1]), peaks[2])
    numerator = jnp.zeros_like(leaf_sum)
    denominator = jnp.zeros_like(leaf_weight)
    for summed, weight_sum, part_peak in zip(sums, weights, peaks):
        scaled = jnp.exp(part_peak - peak)
        numerator = numerator + scaled[..., None] * summed
        denominator = denominator + scaled * weight_sum
    attended = (
        (numerator / denominator[..., None])
        .astype(jnp.bfloat16)
        .reshape(local_leaves, group * head_dim)
    )
    term = jnp.dot(attended, w_output, preferred_element_type=jnp.float32)
    tensor_size = lax.axis_size("tensor")
    pieces = lax.all_to_all(
        term.reshape(local_leaves, tensor_size, term.shape[1] // tensor_size),
        "tensor",
        1,
        1,
        tiled=False,
    )
    mixed = jnp.sum(pieces, 1).astype(jnp.bfloat16)
    return (mixed, new_entry[:, None, :])


def solution(mesh):
    tensor_size = mesh.shape["tensor"]
    request_size = mesh.shape["request"]
    core_size = 2
    y_size = 4
    z_size = request_size // (y_size * core_size)
    fine = Mesh(
        mesh.devices.reshape(tensor_size, z_size, y_size, core_size),
        ("tensor", "z", "y", "core"),
    )
    request = ("z", "y", "core")
    in_specs = (
        P(request, None),
        P(),
        P(None, "tensor"),
        P(None, "tensor"),
        P("tensor", None),
        P(request, "tensor", None, None),
        P(request, "tensor", None, None),
        P(),
        P(),
        P(),
        P(),
        P(),
        P(),
        P(request),
    )
    out_specs = (P(request, "tensor"), P(request, "tensor", None))
    return jax.shard_map(local, mesh=fine, in_specs=in_specs, out_specs=out_specs, check_vma=False)
```

```python
import jax
import jax.numpy as jnp
from jax import lax
from jax.sharding import Mesh, PartitionSpec as P

FLOOR = -1e30


def rotate(values_in, positions):
    half_dim = values_in.shape[-1] // 2
    inverse_freq = 10000.0 ** (
        -(jnp.arange(half_dim, dtype=jnp.float32) * 2.0 / values_in.shape[-1])
    )
    angles = positions.astype(jnp.float32)[..., None] * inverse_freq
    angles = jnp.concatenate([angles, angles], -1)
    turned = jnp.concatenate([-values_in[..., half_dim:], values_in[..., :half_dim]], -1)
    return values_in * jnp.cos(angles) + turned * jnp.sin(angles)


def soft_part(scores, usable, value_rows, pattern):
    scores = jnp.where(usable, scores, FLOOR)
    peak = jnp.max(scores, -1)
    weights = jnp.where(usable, jnp.exp(scores - peak[..., None]), 0.0).astype(jnp.bfloat16)
    summed = jnp.einsum(pattern, weights, value_rows, preferred_element_type=jnp.float32)
    weight_sum = jnp.sum(weights.astype(jnp.float32), -1)
    return (summed, weight_sum, peak)


def split_two(values):
    high = values.astype(jnp.bfloat16)
    low = (values - high.astype(jnp.float32)).astype(jnp.bfloat16)
    return [high, low]


def split_three(values):
    high = values.astype(jnp.bfloat16)
    rest = values - high.astype(jnp.float32)
    middle = rest.astype(jnp.bfloat16)
    low = (rest - middle.astype(jnp.float32)).astype(jnp.bfloat16)
    return [high, middle, low]


def join(pieces):
    total = pieces[0].astype(jnp.float32)
    for piece in pieces[1:]:
        total = total + piece.astype(jnp.float32)
    return total


def group_size(axes):
    size = 1
    for axis in axes if isinstance(axes, tuple) else (axes,):
        size = size * lax.axis_size(axis)
    return size


def gather_rows(values, axes):
    count = group_size(axes)
    spread = jnp.broadcast_to(values[None], (count,) + values.shape)
    received = lax.all_to_all(spread, axes, 0, 0, tiled=False)
    return received.reshape(count * values.shape[0], values.shape[1])


def scatter_rows(values, axes):
    count = group_size(axes)
    blocks = values.reshape(count, values.shape[0] // count, values.shape[1])
    received = lax.all_to_all(blocks, axes, 0, 0, tiled=False)
    return jnp.sum(received.astype(jnp.float32), 0).astype(values.dtype)


def local(
    hidden,
    norm_gain,
    w_query,
    w_keyval,
    w_output,
    node_cache,
    leaf_cache,
    leaf_branch,
    branch_root,
    root_owner,
    branch_owner,
    root_len,
    branch_len,
    leaf_len,
):
    head_dim = w_keyval.shape[1] // 2
    local_leaves = hidden.shape[0]
    group = w_query.shape[1] // head_dim
    factor = head_dim ** (-0.5)
    device = (
        lax.axis_index("z") * (lax.axis_size("y") * lax.axis_size("core"))
        + lax.axis_index("y") * lax.axis_size("core")
        + lax.axis_index("core")
    )
    offset = device * local_leaves
    widened = hidden.astype(jnp.float32)
    normed = (
        widened * lax.rsqrt(jnp.mean(widened * widened, -1, keepdims=True) + 1e-05) * norm_gain
    ).astype(jnp.bfloat16)
    branch_ids = jnp.arange(branch_root.shape[0], dtype=jnp.int32)
    root_ids = jnp.arange(root_owner.shape[0], dtype=jnp.int32)
    own_branch = lax.dynamic_slice_in_dim(leaf_branch, offset, local_leaves)
    own_hits = own_branch[:, None] == branch_ids[None, :]
    own_root = jnp.sum(jnp.where(own_hits, branch_root[None, :], 0), 1)
    positions = (
        jnp.sum(jnp.where(own_root[:, None] == root_ids[None, :], root_len[None, :], 0), 1)
        + jnp.sum(jnp.where(own_hits, branch_len[None, :], 0), 1)
        + leaf_len
    )
    raw_query = jnp.dot(normed, w_query, preferred_element_type=jnp.float32).reshape(
        local_leaves, group, head_dim
    )
    queries = rotate(raw_query, positions[:, None]).astype(jnp.bfloat16)
    everyone = gather_rows(queries.reshape(local_leaves, group * head_dim), ("y", "core"))
    node_rows = node_cache[0, 0]
    slots = gather_rows(node_rows, "z").reshape(-1, node_rows.shape[0], node_rows.shape[1])
    raw_entry = jnp.dot(normed, w_keyval, preferred_element_type=jnp.float32)
    new_entry = jnp.concatenate(
        [rotate(raw_entry[:, :head_dim], positions), raw_entry[:, head_dim:]], -1
    ).astype(jnp.bfloat16)
    leaf_rows = leaf_cache[:, 0]
    slot_index = jnp.arange(leaf_rows.shape[1], dtype=jnp.int32)
    appended = jnp.where(
        (slot_index[None, :] == leaf_len[:, None])[:, :, None], new_entry[:, None, :], leaf_rows
    )
    leaf_scores = (
        jnp.einsum(
            "lgd,lkd->lgk", queries, appended[:, :, :head_dim], preferred_element_type=jnp.float32
        )
        * factor
    )
    leaf_usable = (slot_index[None, :] <= leaf_len[:, None])[:, None, :]
    leaf_sum, leaf_weight, leaf_peak = soft_part(
        leaf_scores, leaf_usable, appended[:, :, head_dim:], "lgk,lkd->lgd"
    )

    row_count = everyone.shape[0]
    slot_count = slots.shape[0]
    y_core_size = row_count // local_leaves
    my_y_core = device % y_core_size
    row_branch = lax.dynamic_slice_in_dim(
        leaf_branch, (device - my_y_core) * local_leaves, row_count
    )
    slot_ids = my_y_core + y_core_size * jnp.arange(slot_count, dtype=jnp.int32)
    branch_root_hits = branch_root[:, None] == root_ids[None, :]
    root_slot_of_branch = jnp.any(
        branch_root_hits[:, None, :] & (root_owner[None, None, :] == slot_ids[None, :, None]), 2
    )
    branch_slot_of_branch = branch_owner[:, None] == slot_ids[None, :]
    row_hits = row_branch[:, None] == branch_ids[None, :]
    root_mine = jnp.any(row_hits[:, :, None] & root_slot_of_branch[None, :, :], 1)
    branch_mine = jnp.any(row_hits[:, :, None] & branch_slot_of_branch[None, :, :], 1)
    mine_all = root_mine | branch_mine
    slot_length = jnp.sum(
        jnp.where(root_owner[None, :] == slot_ids[:, None], root_len[None, :], 0), 1
    ) + jnp.sum(jnp.where(branch_owner[None, :] == slot_ids[:, None], branch_len[None, :], 0), 1)
    node_usable = (
        jnp.arange(slots.shape[1], dtype=jnp.int32)[None, :] < slot_length[:, None]
    )
    rows_query = everyone.reshape(row_count, group, head_dim)
    scores = (
        jnp.einsum(
            "ngd,skd->nsgk", rows_query, slots[:, :, :head_dim], preferred_element_type=jnp.float32
        )
        * factor
    )
    usable = mine_all[:, :, None, None] & node_usable[None, :, None, :]
    slot_sum, slot_weight, slot_peak = soft_part(
        scores, usable, slots[:, :, head_dim:], "nsgk,skd->nsgd"
    )
    slot_peak = jnp.where(mine_all[:, :, None], slot_peak, 0.0)

    def pick(mask, values):
        shape = mask.shape + (1,) * (values.ndim - mask.ndim)
        return jnp.sum(jnp.where(mask.reshape(shape), values, 0.0), 1)

    parts = [
        (pick(mask, slot_sum), pick(mask, slot_weight), pick(mask, slot_peak))
        for mask in (root_mine, branch_mine)
    ]
    pieces = []
    stats = []
    for part_sum, part_weight, part_peak in parts:
        pieces.append(part_sum.reshape(row_count, group * head_dim).astype(jnp.bfloat16))
        stats.append(jnp.concatenate(split_two(part_weight) + split_three(part_peak), -1))
    stat_width = stats[0].shape[1]
    pad_width = (-(2 * group * head_dim + 2 * stat_width)) % 128
    packet = jnp.concatenate(
        pieces + stats + [jnp.zeros((row_count, pad_width), jnp.bfloat16)], -1
    )
    gathered = scatter_rows(packet, ("y", "core"))
    sums = []
    weights = []
    peaks = []
    for part in range(2):
        sums.append(
            gathered[:, part * group * head_dim : (part + 1) * group * head_dim]
            .astype(jnp.float32)
            .reshape(local_leaves, group, head_dim)
        )
        base = 2 * group * head_dim + part * stat_width
        weights.append(join([gathered[:, base + k * group : base + (k + 1) * group] for k in range(2)]))
        base = base + 2 * group
        peaks.append(join([gathered[:, base + k * group : base + (k + 1) * group] for k in range(3)]))
    sums.append(leaf_sum)
    weights.append(leaf_weight)
    peaks.append(leaf_peak)
    peak = jnp.maximum(jnp.maximum(peaks[0], peaks[1]), peaks[2])
    numerator = jnp.zeros_like(leaf_sum)
    denominator = jnp.zeros_like(leaf_weight)
    for summed, weight_sum, part_peak in zip(sums, weights, peaks):
        scaled = jnp.exp(part_peak - peak)
        numerator = numerator + scaled[..., None] * summed
        denominator = denominator + scaled * weight_sum
    attended = (
        (numerator / denominator[..., None])
        .astype(jnp.bfloat16)
        .reshape(local_leaves, group * head_dim)
    )
    term = jnp.dot(attended, w_output, preferred_element_type=jnp.float32)
    tensor_size = lax.axis_size("tensor")
    pieces = lax.all_to_all(
        term.reshape(local_leaves, tensor_size, term.shape[1] // tensor_size),
        "tensor",
        1,
        1,
        tiled=False,
    )
    mixed = jnp.sum(pieces, 1).astype(jnp.bfloat16)
    return (mixed, new_entry[:, None, :])


def solution(mesh):
    tensor_size = mesh.shape["tensor"]
    request_size = mesh.shape["request"]
    core_size = 2
    y_size = 4
    z_size = request_size // (y_size * core_size)
    fine = Mesh(
        mesh.devices.reshape(tensor_size, z_size, y_size, core_size),
        ("tensor", "z", "y", "core"),
    )
    request = ("z", "y", "core")
    in_specs = (
        P(request, None),
        P(),
        P(None, "tensor"),
        P(None, "tensor"),
        P("tensor", None),
        P(request, "tensor", None, None),
        P(request, "tensor", None, None),
        P(),
        P(),
        P(),
        P(),
        P(),
        P(),
        P(request),
    )
    out_specs = (P(request, "tensor"), P(request, "tensor", None))
    return jax.shard_map(local, mesh=fine, in_specs=in_specs, out_specs=out_specs, check_vma=False)
```

```python
import jax
import jax.numpy as jnp
from jax import lax
from jax.sharding import Mesh, PartitionSpec as P

FLOOR = -1e30


def rotate(values_in, positions):
    half_dim = values_in.shape[-1] // 2
    inverse_freq = 10000.0 ** (
        -(jnp.arange(half_dim, dtype=jnp.float32) * 2.0 / values_in.shape[-1])
    )
    angles = positions.astype(jnp.float32)[..., None] * inverse_freq
    angles = jnp.concatenate([angles, angles], -1)
    turned = jnp.concatenate([-values_in[..., half_dim:], values_in[..., :half_dim]], -1)
    return values_in * jnp.cos(angles) + turned * jnp.sin(angles)


def soft_part(scores, usable, value_rows, pattern):
    scores = jnp.where(usable, scores, FLOOR)
    peak = jnp.max(scores, -1)
    weights = jnp.where(usable, jnp.exp(scores - peak[..., None]), 0.0).astype(jnp.bfloat16)
    summed = jnp.einsum(pattern, weights, value_rows, preferred_element_type=jnp.float32)
    weight_sum = jnp.sum(weights.astype(jnp.float32), -1)
    return (summed, weight_sum, peak)


def split_two(values):
    high = values.astype(jnp.bfloat16)
    low = (values - high.astype(jnp.float32)).astype(jnp.bfloat16)
    return [high, low]


def split_three(values):
    high = values.astype(jnp.bfloat16)
    rest = values - high.astype(jnp.float32)
    middle = rest.astype(jnp.bfloat16)
    low = (rest - middle.astype(jnp.float32)).astype(jnp.bfloat16)
    return [high, middle, low]


def join(pieces):
    total = pieces[0].astype(jnp.float32)
    for piece in pieces[1:]:
        total = total + piece.astype(jnp.float32)
    return total


def group_size(axes):
    size = 1
    for axis in axes if isinstance(axes, tuple) else (axes,):
        size = size * lax.axis_size(axis)
    return size


def gather_rows(values, axes):
    count = group_size(axes)
    spread = jnp.broadcast_to(values[None], (count,) + values.shape)
    received = lax.all_to_all(spread, axes, 0, 0, tiled=False)
    return received.reshape(count * values.shape[0], values.shape[1])


def scatter_rows(values, axes):
    count = group_size(axes)
    blocks = values.reshape(count, values.shape[0] // count, values.shape[1])
    received = lax.all_to_all(blocks, axes, 0, 0, tiled=False)
    return jnp.sum(received.astype(jnp.float32), 0).astype(values.dtype)


def local(
    hidden,
    norm_gain,
    w_query,
    w_keyval,
    w_output,
    node_cache,
    leaf_cache,
    leaf_branch,
    branch_root,
    root_owner,
    branch_owner,
    root_len,
    branch_len,
    leaf_len,
):
    head_dim = w_keyval.shape[1] // 2
    local_leaves = hidden.shape[0]
    group = w_query.shape[1] // head_dim
    factor = head_dim ** (-0.5)
    device = (
        lax.axis_index("z") * (lax.axis_size("y") * lax.axis_size("core"))
        + lax.axis_index("y") * lax.axis_size("core")
        + lax.axis_index("core")
    )
    offset = device * local_leaves
    widened = hidden.astype(jnp.float32)
    normed = (
        widened * lax.rsqrt(jnp.mean(widened * widened, -1, keepdims=True) + 1e-05) * norm_gain
    ).astype(jnp.bfloat16)
    branch_ids = jnp.arange(branch_root.shape[0], dtype=jnp.int32)
    root_ids = jnp.arange(root_owner.shape[0], dtype=jnp.int32)
    own_branch = lax.dynamic_slice_in_dim(leaf_branch, offset, local_leaves)
    own_hits = own_branch[:, None] == branch_ids[None, :]
    own_root = jnp.sum(jnp.where(own_hits, branch_root[None, :], 0), 1)
    positions = (
        jnp.sum(jnp.where(own_root[:, None] == root_ids[None, :], root_len[None, :], 0), 1)
        + jnp.sum(jnp.where(own_hits, branch_len[None, :], 0), 1)
        + leaf_len
    )
    raw_query = jnp.dot(normed, w_query, preferred_element_type=jnp.float32).reshape(
        local_leaves, group, head_dim
    )
    queries = rotate(raw_query, positions[:, None]).astype(jnp.bfloat16)
    everyone = gather_rows(queries.reshape(local_leaves, group * head_dim), "z")
    node_rows = node_cache[0, 0]
    slot_count = lax.axis_size("y") * lax.axis_size("core")
    slots = jnp.stack(
        [node_rows]
        + [
            lax.ppermute(
                node_rows,
                ("y", "core"),
                [(source, (source + shift) % slot_count) for source in range(slot_count)],
            )
            for shift in range(1, slot_count)
        ]
    )
    raw_entry = jnp.dot(normed, w_keyval, preferred_element_type=jnp.float32)
    new_entry = jnp.concatenate(
        [rotate(raw_entry[:, :head_dim], positions), raw_entry[:, head_dim:]], -1
    ).astype(jnp.bfloat16)
    leaf_rows = leaf_cache[:, 0]
    slot_index = jnp.arange(leaf_rows.shape[1], dtype=jnp.int32)
    appended = jnp.where(
        (slot_index[None, :] == leaf_len[:, None])[:, :, None], new_entry[:, None, :], leaf_rows
    )
    leaf_scores = (
        jnp.einsum(
            "lgd,lkd->lgk", queries, appended[:, :, :head_dim], preferred_element_type=jnp.float32
        )
        * factor
    )
    leaf_usable = (slot_index[None, :] <= leaf_len[:, None])[:, None, :]
    leaf_sum, leaf_weight, leaf_peak = soft_part(
        leaf_scores, leaf_usable, appended[:, :, head_dim:], "lgk,lkd->lgd"
    )

    row_count = everyone.shape[0]
    z_size = lax.axis_size("z")
    my_y_core = device % slot_count
    first_slot = device - my_y_core
    row_branch = lax.dynamic_slice_in_dim(
        leaf_branch.reshape(z_size, slot_count * local_leaves),
        my_y_core * local_leaves,
        local_leaves,
        axis=1,
    ).reshape(row_count)
    slot_ids = first_slot + (my_y_core - jnp.arange(slot_count, dtype=jnp.int32)) % slot_count
    branch_root_hits = branch_root[:, None] == root_ids[None, :]
    root_slot_of_branch = jnp.any(
        branch_root_hits[:, None, :] & (root_owner[None, None, :] == slot_ids[None, :, None]), 2
    )
    branch_slot_of_branch = branch_owner[:, None] == slot_ids[None, :]
    row_hits = row_branch[:, None] == branch_ids[None, :]
    root_mine = jnp.any(row_hits[:, :, None] & root_slot_of_branch[None, :, :], 1)
    branch_mine = jnp.any(row_hits[:, :, None] & branch_slot_of_branch[None, :, :], 1)
    mine_all = root_mine | branch_mine
    slot_length = jnp.sum(
        jnp.where(root_owner[None, :] == slot_ids[:, None], root_len[None, :], 0), 1
    ) + jnp.sum(jnp.where(branch_owner[None, :] == slot_ids[:, None], branch_len[None, :], 0), 1)
    node_usable = (
        jnp.arange(slots.shape[1], dtype=jnp.int32)[None, :] < slot_length[:, None]
    )
    rows_query = everyone.reshape(row_count, group, head_dim)
    scores = (
        jnp.einsum(
            "ngd,skd->nsgk", rows_query, slots[:, :, :head_dim], preferred_element_type=jnp.float32
        )
        * factor
    )
    usable = mine_all[:, :, None, None] & node_usable[None, :, None, :]
    slot_sum, slot_weight, slot_peak = soft_part(
        scores, usable, slots[:, :, head_dim:], "nsgk,skd->nsgd"
    )
    slot_peak = jnp.where(mine_all[:, :, None], slot_peak, 0.0)

    def pick(mask, values):
        shape = mask.shape + (1,) * (values.ndim - mask.ndim)
        return jnp.sum(jnp.where(mask.reshape(shape), values, 0.0), 1)

    parts = [
        (pick(mask, slot_sum), pick(mask, slot_weight), pick(mask, slot_peak))
        for mask in (root_mine, branch_mine)
    ]
    pieces = []
    stats = []
    for part_sum, part_weight, part_peak in parts:
        pieces.append(part_sum.reshape(row_count, group * head_dim).astype(jnp.bfloat16))
        stats.append(jnp.concatenate(split_two(part_weight) + split_three(part_peak), -1))
    stat_width = stats[0].shape[1]
    pad_width = (-(2 * group * head_dim + 2 * stat_width)) % 128
    packet = jnp.concatenate(
        pieces + stats + [jnp.zeros((row_count, pad_width), jnp.bfloat16)], -1
    )
    gathered = scatter_rows(packet, "z")
    sums = []
    weights = []
    peaks = []
    for part in range(2):
        sums.append(
            gathered[:, part * group * head_dim : (part + 1) * group * head_dim]
            .astype(jnp.float32)
            .reshape(local_leaves, group, head_dim)
        )
        base = 2 * group * head_dim + part * stat_width
        weights.append(join([gathered[:, base + k * group : base + (k + 1) * group] for k in range(2)]))
        base = base + 2 * group
        peaks.append(join([gathered[:, base + k * group : base + (k + 1) * group] for k in range(3)]))
    sums.append(leaf_sum)
    weights.append(leaf_weight)
    peaks.append(leaf_peak)
    peak = jnp.maximum(jnp.maximum(peaks[0], peaks[1]), peaks[2])
    numerator = jnp.zeros_like(leaf_sum)
    denominator = jnp.zeros_like(leaf_weight)
    for summed, weight_sum, part_peak in zip(sums, weights, peaks):
        scaled = jnp.exp(part_peak - peak)
        numerator = numerator + scaled[..., None] * summed
        denominator = denominator + scaled * weight_sum
    attended = (
        (numerator / denominator[..., None])
        .astype(jnp.bfloat16)
        .reshape(local_leaves, group * head_dim)
    )
    term = jnp.dot(attended, w_output, preferred_element_type=jnp.float32)
    tensor_size = lax.axis_size("tensor")
    pieces = lax.all_to_all(
        term.reshape(local_leaves, tensor_size, term.shape[1] // tensor_size),
        "tensor",
        1,
        1,
        tiled=False,
    )
    mixed = jnp.sum(pieces, 1).astype(jnp.bfloat16)
    return (mixed, new_entry[:, None, :])


def solution(mesh):
    tensor_size = mesh.shape["tensor"]
    request_size = mesh.shape["request"]
    core_size = 2
    y_size = 4
    z_size = request_size // (y_size * core_size)
    fine = Mesh(
        mesh.devices.reshape(tensor_size, z_size, y_size, core_size),
        ("tensor", "z", "y", "core"),
    )
    request = ("z", "y", "core")
    in_specs = (
        P(request, None),
        P(),
        P(None, "tensor"),
        P(None, "tensor"),
        P("tensor", None),
        P(request, "tensor", None, None),
        P(request, "tensor", None, None),
        P(),
        P(),
        P(),
        P(),
        P(),
        P(),
        P(request),
    )
    out_specs = (P(request, "tensor"), P(request, "tensor", None))
    return jax.shard_map(local, mesh=fine, in_specs=in_specs, out_specs=out_specs, check_vma=False)
```

```python
import jax
import jax.numpy as jnp
from jax import lax
from jax.sharding import Mesh, PartitionSpec as P

FLOOR = -1e30


def rotate(values_in, positions):
    half_dim = values_in.shape[-1] // 2
    inverse_freq = 10000.0 ** (
        -(jnp.arange(half_dim, dtype=jnp.float32) * 2.0 / values_in.shape[-1])
    )
    angles = positions.astype(jnp.float32)[..., None] * inverse_freq
    angles = jnp.concatenate([angles, angles], -1)
    turned = jnp.concatenate([-values_in[..., half_dim:], values_in[..., :half_dim]], -1)
    return values_in * jnp.cos(angles) + turned * jnp.sin(angles)


def soft_part(scores, usable, value_rows, pattern):
    scores = jnp.where(usable, scores, FLOOR)
    peak = jnp.max(scores, -1)
    weights = jnp.where(usable, jnp.exp(scores - peak[..., None]), 0.0).astype(jnp.bfloat16)
    summed = jnp.einsum(pattern, weights, value_rows, preferred_element_type=jnp.float32)
    weight_sum = jnp.sum(weights.astype(jnp.float32), -1)
    return (summed, weight_sum, peak)


def split_two(values):
    high = values.astype(jnp.bfloat16)
    low = (values - high.astype(jnp.float32)).astype(jnp.bfloat16)
    return [high, low]


def split_three(values):
    high = values.astype(jnp.bfloat16)
    rest = values - high.astype(jnp.float32)
    middle = rest.astype(jnp.bfloat16)
    low = (rest - middle.astype(jnp.float32)).astype(jnp.bfloat16)
    return [high, middle, low]


def join(pieces):
    total = pieces[0].astype(jnp.float32)
    for piece in pieces[1:]:
        total = total + piece.astype(jnp.float32)
    return total


def group_size(axes):
    size = 1
    for axis in axes if isinstance(axes, tuple) else (axes,):
        size = size * lax.axis_size(axis)
    return size


def gather_rows(values, axes):
    count = group_size(axes)
    spread = jnp.broadcast_to(values[None], (count,) + values.shape)
    received = lax.all_to_all(spread, axes, 0, 0, tiled=False)
    return received.reshape(count * values.shape[0], values.shape[1])


def scatter_rows(values, axes):
    count = group_size(axes)
    blocks = values.reshape(count, values.shape[0] // count, values.shape[1])
    received = lax.all_to_all(blocks, axes, 0, 0, tiled=False)
    return jnp.sum(received.astype(jnp.float32), 0).astype(values.dtype)


def local(
    hidden,
    norm_gain,
    w_query,
    w_keyval,
    w_output,
    node_cache,
    leaf_cache,
    leaf_branch,
    branch_root,
    root_owner,
    branch_owner,
    root_len,
    branch_len,
    leaf_len,
):
    head_dim = w_keyval.shape[1] // 2
    local_leaves = hidden.shape[0]
    group = w_query.shape[1] // head_dim
    factor = head_dim ** (-0.5)
    device = (
        lax.axis_index("z") * (lax.axis_size("y") * lax.axis_size("core"))
        + lax.axis_index("y") * lax.axis_size("core")
        + lax.axis_index("core")
    )
    offset = device * local_leaves
    widened = hidden.astype(jnp.float32)
    normed = (
        widened * lax.rsqrt(jnp.mean(widened * widened, -1, keepdims=True) + 1e-05) * norm_gain
    ).astype(jnp.bfloat16)
    branch_ids = jnp.arange(branch_root.shape[0], dtype=jnp.int32)
    root_ids = jnp.arange(root_owner.shape[0], dtype=jnp.int32)
    own_branch = lax.dynamic_slice_in_dim(leaf_branch, offset, local_leaves)
    own_hits = own_branch[:, None] == branch_ids[None, :]
    own_root = jnp.sum(jnp.where(own_hits, branch_root[None, :], 0), 1)
    positions = (
        jnp.sum(jnp.where(own_root[:, None] == root_ids[None, :], root_len[None, :], 0), 1)
        + jnp.sum(jnp.where(own_hits, branch_len[None, :], 0), 1)
        + leaf_len
    )
    raw_query = jnp.dot(normed, w_query, preferred_element_type=jnp.float32).reshape(
        local_leaves, group, head_dim
    )
    queries = rotate(raw_query, positions[:, None]).astype(jnp.bfloat16)
    node_rows = node_cache[0, 0]
    slots = gather_rows(node_rows, ("y", "core")).reshape(
        -1, node_rows.shape[0], node_rows.shape[1]
    )
    queries, slots = lax.optimization_barrier((queries, slots))
    everyone = gather_rows(queries.reshape(local_leaves, group * head_dim), "z")
    raw_entry = jnp.dot(normed, w_keyval, preferred_element_type=jnp.float32)
    new_entry = jnp.concatenate(
        [rotate(raw_entry[:, :head_dim], positions), raw_entry[:, head_dim:]], -1
    ).astype(jnp.bfloat16)
    leaf_rows = leaf_cache[:, 0]
    slot_index = jnp.arange(leaf_rows.shape[1], dtype=jnp.int32)
    appended = jnp.where(
        (slot_index[None, :] == leaf_len[:, None])[:, :, None], new_entry[:, None, :], leaf_rows
    )
    leaf_scores = (
        jnp.einsum(
            "lgd,lkd->lgk", queries, appended[:, :, :head_dim], preferred_element_type=jnp.float32
        )
        * factor
    )
    leaf_usable = (slot_index[None, :] <= leaf_len[:, None])[:, None, :]
    leaf_sum, leaf_weight, leaf_peak = soft_part(
        leaf_scores, leaf_usable, appended[:, :, head_dim:], "lgk,lkd->lgd"
    )

    row_count = everyone.shape[0]
    slot_count = slots.shape[0]
    z_size = lax.axis_size("z")
    my_y_core = device % slot_count
    first_slot = device - my_y_core
    row_branch = lax.dynamic_slice_in_dim(
        leaf_branch.reshape(z_size, slot_count * local_leaves),
        my_y_core * local_leaves,
        local_leaves,
        axis=1,
    ).reshape(row_count)
    slot_ids = first_slot + jnp.arange(slot_count, dtype=jnp.int32)
    branch_root_hits = branch_root[:, None] == root_ids[None, :]
    root_slot_of_branch = jnp.any(
        branch_root_hits[:, None, :] & (root_owner[None, None, :] == slot_ids[None, :, None]), 2
    )
    branch_slot_of_branch = branch_owner[:, None] == slot_ids[None, :]
    row_hits = row_branch[:, None] == branch_ids[None, :]
    root_mine = jnp.any(row_hits[:, :, None] & root_slot_of_branch[None, :, :], 1)
    branch_mine = jnp.any(row_hits[:, :, None] & branch_slot_of_branch[None, :, :], 1)
    mine_all = root_mine | branch_mine
    slot_length = jnp.sum(
        jnp.where(root_owner[None, :] == slot_ids[:, None], root_len[None, :], 0), 1
    ) + jnp.sum(jnp.where(branch_owner[None, :] == slot_ids[:, None], branch_len[None, :], 0), 1)
    node_usable = (
        jnp.arange(slots.shape[1], dtype=jnp.int32)[None, :] < slot_length[:, None]
    )
    rows_query = everyone.reshape(row_count, group, head_dim)
    scores = (
        jnp.einsum(
            "ngd,skd->nsgk", rows_query, slots[:, :, :head_dim], preferred_element_type=jnp.float32
        )
        * factor
    )
    usable = mine_all[:, :, None, None] & node_usable[None, :, None, :]
    slot_sum, slot_weight, slot_peak = soft_part(
        scores, usable, slots[:, :, head_dim:], "nsgk,skd->nsgd"
    )
    slot_peak = jnp.where(mine_all[:, :, None], slot_peak, 0.0)

    def pick(mask, values):
        shape = mask.shape + (1,) * (values.ndim - mask.ndim)
        return jnp.sum(jnp.where(mask.reshape(shape), values, 0.0), 1)

    parts = [
        (pick(mask, slot_sum), pick(mask, slot_weight), pick(mask, slot_peak))
        for mask in (root_mine, branch_mine)
    ]
    pieces = []
    stats = []
    for part_sum, part_weight, part_peak in parts:
        pieces.append(part_sum.reshape(row_count, group * head_dim).astype(jnp.bfloat16))
        stats.append(jnp.concatenate(split_two(part_weight) + split_three(part_peak), -1))
    stat_width = stats[0].shape[1]
    pad_width = (-(2 * group * head_dim + 2 * stat_width)) % 128
    packet = jnp.concatenate(
        pieces + stats + [jnp.zeros((row_count, pad_width), jnp.bfloat16)], -1
    )
    gathered = scatter_rows(packet, "z")
    sums = []
    weights = []
    peaks = []
    for part in range(2):
        sums.append(
            gathered[:, part * group * head_dim : (part + 1) * group * head_dim]
            .astype(jnp.float32)
            .reshape(local_leaves, group, head_dim)
        )
        base = 2 * group * head_dim + part * stat_width
        weights.append(join([gathered[:, base + k * group : base + (k + 1) * group] for k in range(2)]))
        base = base + 2 * group
        peaks.append(join([gathered[:, base + k * group : base + (k + 1) * group] for k in range(3)]))
    sums.append(leaf_sum)
    weights.append(leaf_weight)
    peaks.append(leaf_peak)
    peak = jnp.maximum(jnp.maximum(peaks[0], peaks[1]), peaks[2])
    numerator = jnp.zeros_like(leaf_sum)
    denominator = jnp.zeros_like(leaf_weight)
    for summed, weight_sum, part_peak in zip(sums, weights, peaks):
        scaled = jnp.exp(part_peak - peak)
        numerator = numerator + scaled[..., None] * summed
        denominator = denominator + scaled * weight_sum
    attended = (
        (numerator / denominator[..., None])
        .astype(jnp.bfloat16)
        .reshape(local_leaves, group * head_dim)
    )
    term = jnp.dot(attended, w_output, preferred_element_type=jnp.float32)
    tensor_size = lax.axis_size("tensor")
    pieces = lax.all_to_all(
        term.reshape(local_leaves, tensor_size, term.shape[1] // tensor_size),
        "tensor",
        1,
        1,
        tiled=False,
    )
    mixed = jnp.sum(pieces, 1).astype(jnp.bfloat16)
    return (mixed, new_entry[:, None, :])


def solution(mesh):
    tensor_size = mesh.shape["tensor"]
    request_size = mesh.shape["request"]
    core_size = 2
    y_size = 4
    z_size = request_size // (y_size * core_size)
    fine = Mesh(
        mesh.devices.reshape(tensor_size, z_size, y_size, core_size),
        ("tensor", "z", "y", "core"),
    )
    request = ("z", "y", "core")
    in_specs = (
        P(request, None),
        P(),
        P(None, "tensor"),
        P(None, "tensor"),
        P("tensor", None),
        P(request, "tensor", None, None),
        P(request, "tensor", None, None),
        P(),
        P(),
        P(),
        P(),
        P(),
        P(),
        P(request),
    )
    out_specs = (P(request, "tensor"), P(request, "tensor", None))
    return jax.shard_map(local, mesh=fine, in_specs=in_specs, out_specs=out_specs, check_vma=False)
```

```python
import jax
import jax.numpy as jnp
from jax import lax
from jax.sharding import Mesh, PartitionSpec as P

FLOOR = -1e30


def rotate(values_in, positions):
    half_dim = values_in.shape[-1] // 2
    inverse_freq = 10000.0 ** (
        -(jnp.arange(half_dim, dtype=jnp.float32) * 2.0 / values_in.shape[-1])
    )
    angles = positions.astype(jnp.float32)[..., None] * inverse_freq
    angles = jnp.concatenate([angles, angles], -1)
    turned = jnp.concatenate([-values_in[..., half_dim:], values_in[..., :half_dim]], -1)
    return values_in * jnp.cos(angles) + turned * jnp.sin(angles)


def soft_part(scores, usable, value_rows, pattern):
    scores = jnp.where(usable, scores, FLOOR)
    peak = jnp.max(scores, -1)
    weights = jnp.where(usable, jnp.exp(scores - peak[..., None]), 0.0).astype(jnp.bfloat16)
    summed = jnp.einsum(pattern, weights, value_rows, preferred_element_type=jnp.float32)
    weight_sum = jnp.sum(weights.astype(jnp.float32), -1)
    return (summed, weight_sum, peak)


def split_two(values):
    high = values.astype(jnp.bfloat16)
    low = (values - high.astype(jnp.float32)).astype(jnp.bfloat16)
    return [high, low]


def split_three(values):
    high = values.astype(jnp.bfloat16)
    rest = values - high.astype(jnp.float32)
    middle = rest.astype(jnp.bfloat16)
    low = (rest - middle.astype(jnp.float32)).astype(jnp.bfloat16)
    return [high, middle, low]


def join(pieces):
    total = pieces[0].astype(jnp.float32)
    for piece in pieces[1:]:
        total = total + piece.astype(jnp.float32)
    return total


def group_size(axes):
    size = 1
    for axis in axes if isinstance(axes, tuple) else (axes,):
        size = size * lax.axis_size(axis)
    return size


def gather_rows(values, axes):
    count = group_size(axes)
    spread = jnp.broadcast_to(values[None], (count,) + values.shape)
    received = lax.all_to_all(spread, axes, 0, 0, tiled=False)
    return received.reshape(count * values.shape[0], values.shape[1])


def scatter_rows(values, axes):
    count = group_size(axes)
    blocks = values.reshape(count, values.shape[0] // count, values.shape[1])
    received = lax.all_to_all(blocks, axes, 0, 0, tiled=False)
    return jnp.sum(received.astype(jnp.float32), 0).astype(values.dtype)


def local(
    hidden,
    norm_gain,
    w_query,
    w_keyval,
    w_output,
    node_cache,
    leaf_cache,
    leaf_branch,
    branch_root,
    root_owner,
    branch_owner,
    root_len,
    branch_len,
    leaf_len,
):
    head_dim = w_keyval.shape[1] // 2
    local_leaves = hidden.shape[0]
    group = w_query.shape[1] // head_dim
    factor = head_dim ** (-0.5)
    device = (
        (lax.axis_index("zh") * lax.axis_size("zl") + lax.axis_index("zl"))
        * (lax.axis_size("y") * lax.axis_size("core"))
        + lax.axis_index("y") * lax.axis_size("core")
        + lax.axis_index("core")
    )
    offset = device * local_leaves
    widened = hidden.astype(jnp.float32)
    normed = (
        widened * lax.rsqrt(jnp.mean(widened * widened, -1, keepdims=True) + 1e-05) * norm_gain
    ).astype(jnp.bfloat16)
    branch_ids = jnp.arange(branch_root.shape[0], dtype=jnp.int32)
    root_ids = jnp.arange(root_owner.shape[0], dtype=jnp.int32)
    own_branch = lax.dynamic_slice_in_dim(leaf_branch, offset, local_leaves)
    own_hits = own_branch[:, None] == branch_ids[None, :]
    own_root = jnp.sum(jnp.where(own_hits, branch_root[None, :], 0), 1)
    positions = (
        jnp.sum(jnp.where(own_root[:, None] == root_ids[None, :], root_len[None, :], 0), 1)
        + jnp.sum(jnp.where(own_hits, branch_len[None, :], 0), 1)
        + leaf_len
    )
    raw_query = jnp.dot(normed, w_query, preferred_element_type=jnp.float32).reshape(
        local_leaves, group, head_dim
    )
    queries = rotate(raw_query, positions[:, None]).astype(jnp.bfloat16)
    node_rows = node_cache[0, 0]
    slots = gather_rows(node_rows, ("y", "core")).reshape(
        -1, node_rows.shape[0], node_rows.shape[1]
    )
    queries, slots = lax.optimization_barrier((queries, slots))
    everyone = gather_rows(
        gather_rows(queries.reshape(local_leaves, group * head_dim), "zl"), "zh"
    )
    raw_entry = jnp.dot(normed, w_keyval, preferred_element_type=jnp.float32)
    new_entry = jnp.concatenate(
        [rotate(raw_entry[:, :head_dim], positions), raw_entry[:, head_dim:]], -1
    ).astype(jnp.bfloat16)
    leaf_rows = leaf_cache[:, 0]
    slot_index = jnp.arange(leaf_rows.shape[1], dtype=jnp.int32)
    appended = jnp.where(
        (slot_index[None, :] == leaf_len[:, None])[:, :, None], new_entry[:, None, :], leaf_rows
    )
    leaf_scores = (
        jnp.einsum(
            "lgd,lkd->lgk", queries, appended[:, :, :head_dim], preferred_element_type=jnp.float32
        )
        * factor
    )
    leaf_usable = (slot_index[None, :] <= leaf_len[:, None])[:, None, :]
    leaf_sum, leaf_weight, leaf_peak = soft_part(
        leaf_scores, leaf_usable, appended[:, :, head_dim:], "lgk,lkd->lgd"
    )

    row_count = everyone.shape[0]
    slot_count = slots.shape[0]
    z_size = lax.axis_size("zh") * lax.axis_size("zl")
    my_y_core = device % slot_count
    first_slot = device - my_y_core
    row_branch = lax.dynamic_slice_in_dim(
        leaf_branch.reshape(z_size, slot_count * local_leaves),
        my_y_core * local_leaves,
        local_leaves,
        axis=1,
    ).reshape(row_count)
    slot_ids = first_slot + jnp.arange(slot_count, dtype=jnp.int32)
    branch_root_hits = branch_root[:, None] == root_ids[None, :]
    root_slot_of_branch = jnp.any(
        branch_root_hits[:, None, :] & (root_owner[None, None, :] == slot_ids[None, :, None]), 2
    )
    branch_slot_of_branch = branch_owner[:, None] == slot_ids[None, :]
    row_hits = row_branch[:, None] == branch_ids[None, :]
    root_mine = jnp.any(row_hits[:, :, None] & root_slot_of_branch[None, :, :], 1)
    branch_mine = jnp.any(row_hits[:, :, None] & branch_slot_of_branch[None, :, :], 1)
    mine_all = root_mine | branch_mine
    slot_length = jnp.sum(
        jnp.where(root_owner[None, :] == slot_ids[:, None], root_len[None, :], 0), 1
    ) + jnp.sum(jnp.where(branch_owner[None, :] == slot_ids[:, None], branch_len[None, :], 0), 1)
    node_usable = (
        jnp.arange(slots.shape[1], dtype=jnp.int32)[None, :] < slot_length[:, None]
    )
    rows_query = everyone.reshape(row_count, group, head_dim)
    scores = (
        jnp.einsum(
            "ngd,skd->nsgk", rows_query, slots[:, :, :head_dim], preferred_element_type=jnp.float32
        )
        * factor
    )
    usable = mine_all[:, :, None, None] & node_usable[None, :, None, :]
    slot_sum, slot_weight, slot_peak = soft_part(
        scores, usable, slots[:, :, head_dim:], "nsgk,skd->nsgd"
    )
    slot_peak = jnp.where(mine_all[:, :, None], slot_peak, 0.0)

    def pick(mask, values):
        shape = mask.shape + (1,) * (values.ndim - mask.ndim)
        return jnp.sum(jnp.where(mask.reshape(shape), values, 0.0), 1)

    parts = [
        (pick(mask, slot_sum), pick(mask, slot_weight), pick(mask, slot_peak))
        for mask in (root_mine, branch_mine)
    ]
    pieces = []
    stats = []
    for part_sum, part_weight, part_peak in parts:
        pieces.append(part_sum.reshape(row_count, group * head_dim).astype(jnp.bfloat16))
        stats.append(jnp.concatenate(split_two(part_weight) + split_three(part_peak), -1))
    stat_width = stats[0].shape[1]
    pad_width = (-(2 * group * head_dim + 2 * stat_width)) % 128
    packet = jnp.concatenate(
        pieces + stats + [jnp.zeros((row_count, pad_width), jnp.bfloat16)], -1
    )
    gathered = scatter_rows(scatter_rows(packet, "zh"), "zl")
    sums = []
    weights = []
    peaks = []
    for part in range(2):
        sums.append(
            gathered[:, part * group * head_dim : (part + 1) * group * head_dim]
            .astype(jnp.float32)
            .reshape(local_leaves, group, head_dim)
        )
        base = 2 * group * head_dim + part * stat_width
        weights.append(join([gathered[:, base + k * group : base + (k + 1) * group] for k in range(2)]))
        base = base + 2 * group
        peaks.append(join([gathered[:, base + k * group : base + (k + 1) * group] for k in range(3)]))
    sums.append(leaf_sum)
    weights.append(leaf_weight)
    peaks.append(leaf_peak)
    peak = jnp.maximum(jnp.maximum(peaks[0], peaks[1]), peaks[2])
    numerator = jnp.zeros_like(leaf_sum)
    denominator = jnp.zeros_like(leaf_weight)
    for summed, weight_sum, part_peak in zip(sums, weights, peaks):
        scaled = jnp.exp(part_peak - peak)
        numerator = numerator + scaled[..., None] * summed
        denominator = denominator + scaled * weight_sum
    attended = (
        (numerator / denominator[..., None])
        .astype(jnp.bfloat16)
        .reshape(local_leaves, group * head_dim)
    )
    term = jnp.dot(attended, w_output, preferred_element_type=jnp.float32)
    tensor_size = lax.axis_size("tensor")
    pieces = lax.all_to_all(
        term.reshape(local_leaves, tensor_size, term.shape[1] // tensor_size),
        "tensor",
        1,
        1,
        tiled=False,
    )
    mixed = jnp.sum(pieces, 1).astype(jnp.bfloat16)
    return (mixed, new_entry[:, None, :])


def solution(mesh):
    tensor_size = mesh.shape["tensor"]
    request_size = mesh.shape["request"]
    core_size = 2
    y_size = 4
    z_size = request_size // (y_size * core_size)
    z_low = 4
    fine = Mesh(
        mesh.devices.reshape(tensor_size, z_size // z_low, z_low, y_size, core_size),
        ("tensor", "zh", "zl", "y", "core"),
    )
    request = ("zh", "zl", "y", "core")
    in_specs = (
        P(request, None),
        P(),
        P(None, "tensor"),
        P(None, "tensor"),
        P("tensor", None),
        P(request, "tensor", None, None),
        P(request, "tensor", None, None),
        P(),
        P(),
        P(),
        P(),
        P(),
        P(),
        P(request),
    )
    out_specs = (P(request, "tensor"), P(request, "tensor", None))
    return jax.shard_map(local, mesh=fine, in_specs=in_specs, out_specs=out_specs, check_vma=False)
```

```python
import jax
import jax.numpy as jnp
from jax import lax
from jax.sharding import Mesh, PartitionSpec as P

FLOOR = -1e30


def rotate(values_in, positions):
    half_dim = values_in.shape[-1] // 2
    inverse_freq = 10000.0 ** (
        -(jnp.arange(half_dim, dtype=jnp.float32) * 2.0 / values_in.shape[-1])
    )
    angles = positions.astype(jnp.float32)[..., None] * inverse_freq
    angles = jnp.concatenate([angles, angles], -1)
    turned = jnp.concatenate([-values_in[..., half_dim:], values_in[..., :half_dim]], -1)
    return values_in * jnp.cos(angles) + turned * jnp.sin(angles)


def soft_part(scores, usable, value_rows, pattern):
    scores = jnp.where(usable, scores, FLOOR)
    peak = jnp.max(scores, -1)
    weights = jnp.where(usable, jnp.exp(scores - peak[..., None]), 0.0).astype(jnp.bfloat16)
    summed = jnp.einsum(pattern, weights, value_rows, preferred_element_type=jnp.float32)
    weight_sum = jnp.sum(weights.astype(jnp.float32), -1)
    return (summed, weight_sum, peak)


def split_two(values):
    high = values.astype(jnp.bfloat16)
    low = (values - high.astype(jnp.float32)).astype(jnp.bfloat16)
    return [high, low]


def split_three(values):
    high = values.astype(jnp.bfloat16)
    rest = values - high.astype(jnp.float32)
    middle = rest.astype(jnp.bfloat16)
    low = (rest - middle.astype(jnp.float32)).astype(jnp.bfloat16)
    return [high, middle, low]


def join(pieces):
    total = pieces[0].astype(jnp.float32)
    for piece in pieces[1:]:
        total = total + piece.astype(jnp.float32)
    return total


def group_size(axes):
    size = 1
    for axis in axes if isinstance(axes, tuple) else (axes,):
        size = size * lax.axis_size(axis)
    return size


def gather_rows(values, axes):
    count = group_size(axes)
    spread = jnp.broadcast_to(values[None], (count,) + values.shape)
    received = lax.all_to_all(spread, axes, 0, 0, tiled=False)
    return received.reshape(count * values.shape[0], values.shape[1])


def scatter_rows(values, axes):
    count = group_size(axes)
    blocks = values.reshape(count, values.shape[0] // count, values.shape[1])
    received = lax.all_to_all(blocks, axes, 0, 0, tiled=False)
    return jnp.sum(received.astype(jnp.float32), 0).astype(values.dtype)


def local(
    hidden,
    norm_gain,
    w_query,
    w_keyval,
    w_output,
    node_cache,
    leaf_cache,
    leaf_branch,
    branch_root,
    root_owner,
    branch_owner,
    root_len,
    branch_len,
    leaf_len,
):
    head_dim = w_keyval.shape[1] // 2
    local_leaves = hidden.shape[0]
    group = w_query.shape[1] // head_dim
    factor = head_dim ** (-0.5)
    device = (
        lax.axis_index("z") * (lax.axis_size("y") * lax.axis_size("core"))
        + lax.axis_index("y") * lax.axis_size("core")
        + lax.axis_index("core")
    )
    offset = device * local_leaves
    widened = hidden.astype(jnp.float32)
    normed = (
        widened * lax.rsqrt(jnp.mean(widened * widened, -1, keepdims=True) + 1e-05) * norm_gain
    ).astype(jnp.bfloat16)
    branch_ids = jnp.arange(branch_root.shape[0], dtype=jnp.int32)
    root_ids = jnp.arange(root_owner.shape[0], dtype=jnp.int32)
    own_branch = lax.dynamic_slice_in_dim(leaf_branch, offset, local_leaves)
    own_hits = own_branch[:, None] == branch_ids[None, :]
    own_root = jnp.sum(jnp.where(own_hits, branch_root[None, :], 0), 1)
    positions = (
        jnp.sum(jnp.where(own_root[:, None] == root_ids[None, :], root_len[None, :], 0), 1)
        + jnp.sum(jnp.where(own_hits, branch_len[None, :], 0), 1)
        + leaf_len
    )
    raw_query = jnp.dot(normed, w_query, preferred_element_type=jnp.float32).reshape(
        local_leaves, group, head_dim
    )
    queries = rotate(raw_query, positions[:, None]).astype(jnp.bfloat16)
    node_rows = node_cache[0, 0]
    slots = gather_rows(node_rows, ("y", "core")).reshape(
        -1, node_rows.shape[0], node_rows.shape[1]
    )
    queries, slots = lax.optimization_barrier((queries, slots))
    everyone = gather_rows(queries.reshape(local_leaves, group * head_dim), "z")
    raw_entry = jnp.dot(normed, w_keyval, preferred_element_type=jnp.float32)
    new_entry = jnp.concatenate(
        [rotate(raw_entry[:, :head_dim], positions), raw_entry[:, head_dim:]], -1
    ).astype(jnp.bfloat16)
    leaf_rows = leaf_cache[:, 0]
    slot_index = jnp.arange(leaf_rows.shape[1], dtype=jnp.int32)
    appended = jnp.where(
        (slot_index[None, :] == leaf_len[:, None])[:, :, None], new_entry[:, None, :], leaf_rows
    )
    leaf_scores = (
        jnp.einsum(
            "lgd,lkd->lgk", queries, appended[:, :, :head_dim], preferred_element_type=jnp.float32
        )
        * factor
    )
    leaf_usable = (slot_index[None, :] <= leaf_len[:, None])[:, None, :]
    leaf_sum, leaf_weight, leaf_peak = soft_part(
        leaf_scores, leaf_usable, appended[:, :, head_dim:], "lgk,lkd->lgd"
    )

    row_count = everyone.shape[0]
    slot_count = slots.shape[0]
    z_size = lax.axis_size("z")
    my_y_core = device % slot_count
    first_slot = device - my_y_core
    row_branch = lax.dynamic_slice_in_dim(
        leaf_branch.reshape(z_size, slot_count * local_leaves),
        my_y_core * local_leaves,
        local_leaves,
        axis=1,
    ).reshape(row_count)
    slot_ids = first_slot + jnp.arange(slot_count, dtype=jnp.int32)
    branch_root_hits = branch_root[:, None] == root_ids[None, :]
    root_slot_of_branch = jnp.any(
        branch_root_hits[:, None, :] & (root_owner[None, None, :] == slot_ids[None, :, None]), 2
    )
    branch_slot_of_branch = branch_owner[:, None] == slot_ids[None, :]
    row_hits = row_branch[:, None] == branch_ids[None, :]
    root_mine = jnp.any(row_hits[:, :, None] & root_slot_of_branch[None, :, :], 1)
    branch_mine = jnp.any(row_hits[:, :, None] & branch_slot_of_branch[None, :, :], 1)
    mine_all = root_mine | branch_mine
    slot_length = jnp.sum(
        jnp.where(root_owner[None, :] == slot_ids[:, None], root_len[None, :], 0), 1
    ) + jnp.sum(jnp.where(branch_owner[None, :] == slot_ids[:, None], branch_len[None, :], 0), 1)
    node_usable = (
        jnp.arange(slots.shape[1], dtype=jnp.int32)[None, :] < slot_length[:, None]
    )
    rows_query = everyone.reshape(row_count, group, head_dim)
    scores = (
        jnp.einsum(
            "ngd,skd->nsgk", rows_query, slots[:, :, :head_dim], preferred_element_type=jnp.float32
        )
        * factor
    )
    usable = mine_all[:, :, None, None] & node_usable[None, :, None, :]
    scores = jnp.where(usable, scores, FLOOR)
    slot_peak = jnp.max(scores, -1)
    weights = jnp.where(usable, jnp.exp(scores - slot_peak[..., None]), 0.0).astype(jnp.bfloat16)
    slot_peak = jnp.where(mine_all[:, :, None], slot_peak, 0.0)
    parts = []
    for mask in (root_mine, branch_mine):
        part_weights = jnp.where(mask[:, :, None, None], weights, jnp.zeros_like(weights))
        part_sum = jnp.einsum(
            "nsgk,skd->ngd", part_weights, slots[:, :, head_dim:], preferred_element_type=jnp.float32
        )
        part_weight = jnp.sum(part_weights.astype(jnp.float32), (1, 3))
        part_peak = jnp.sum(jnp.where(mask[:, :, None], slot_peak, 0.0), 1)
        parts.append((part_sum, part_weight, part_peak))
    pieces = []
    stats = []
    for part_sum, part_weight, part_peak in parts:
        pieces.append(part_sum.reshape(row_count, group * head_dim).astype(jnp.bfloat16))
        stats.append(jnp.concatenate(split_two(part_weight) + split_three(part_peak), -1))
    stat_width = stats[0].shape[1]
    pad_width = (-(2 * group * head_dim + 2 * stat_width)) % 128
    packet = jnp.concatenate(
        pieces + stats + [jnp.zeros((row_count, pad_width), jnp.bfloat16)], -1
    )
    gathered = scatter_rows(packet, "z")
    sums = []
    weights = []
    peaks = []
    for part in range(2):
        sums.append(
            gathered[:, part * group * head_dim : (part + 1) * group * head_dim]
            .astype(jnp.float32)
            .reshape(local_leaves, group, head_dim)
        )
        base = 2 * group * head_dim + part * stat_width
        weights.append(join([gathered[:, base + k * group : base + (k + 1) * group] for k in range(2)]))
        base = base + 2 * group
        peaks.append(join([gathered[:, base + k * group : base + (k + 1) * group] for k in range(3)]))
    sums.append(leaf_sum)
    weights.append(leaf_weight)
    peaks.append(leaf_peak)
    peak = jnp.maximum(jnp.maximum(peaks[0], peaks[1]), peaks[2])
    numerator = jnp.zeros_like(leaf_sum)
    denominator = jnp.zeros_like(leaf_weight)
    for summed, weight_sum, part_peak in zip(sums, weights, peaks):
        scaled = jnp.exp(part_peak - peak)
        numerator = numerator + scaled[..., None] * summed
        denominator = denominator + scaled * weight_sum
    attended = (
        (numerator / denominator[..., None])
        .astype(jnp.bfloat16)
        .reshape(local_leaves, group * head_dim)
    )
    term = jnp.dot(attended, w_output, preferred_element_type=jnp.float32)
    tensor_size = lax.axis_size("tensor")
    pieces = lax.all_to_all(
        term.reshape(local_leaves, tensor_size, term.shape[1] // tensor_size),
        "tensor",
        1,
        1,
        tiled=False,
    )
    mixed = jnp.sum(pieces, 1).astype(jnp.bfloat16)
    return (mixed, new_entry[:, None, :])


def solution(mesh):
    tensor_size = mesh.shape["tensor"]
    request_size = mesh.shape["request"]
    core_size = 2
    y_size = 4
    z_size = request_size // (y_size * core_size)
    fine = Mesh(
        mesh.devices.reshape(tensor_size, z_size, y_size, core_size),
        ("tensor", "z", "y", "core"),
    )
    request = ("z", "y", "core")
    in_specs = (
        P(request, None),
        P(),
        P(None, "tensor"),
        P(None, "tensor"),
        P("tensor", None),
        P(request, "tensor", None, None),
        P(request, "tensor", None, None),
        P(),
        P(),
        P(),
        P(),
        P(),
        P(),
        P(request),
    )
    out_specs = (P(request, "tensor"), P(request, "tensor", None))
    return jax.shard_map(local, mesh=fine, in_specs=in_specs, out_specs=out_specs, check_vma=False)
```

```python
import jax
import jax.numpy as jnp
from jax import lax
from jax.sharding import Mesh, PartitionSpec as P

FLOOR = -1e30


def rotate(values_in, positions):
    half_dim = values_in.shape[-1] // 2
    inverse_freq = 10000.0 ** (
        -(jnp.arange(half_dim, dtype=jnp.float32) * 2.0 / values_in.shape[-1])
    )
    angles = positions.astype(jnp.float32)[..., None] * inverse_freq
    angles = jnp.concatenate([angles, angles], -1)
    turned = jnp.concatenate([-values_in[..., half_dim:], values_in[..., :half_dim]], -1)
    return values_in * jnp.cos(angles) + turned * jnp.sin(angles)


def soft_part(scores, usable, value_rows, pattern):
    scores = jnp.where(usable, scores, FLOOR)
    peak = jnp.max(scores, -1)
    weights = jnp.where(usable, jnp.exp(scores - peak[..., None]), 0.0).astype(jnp.bfloat16)
    summed = jnp.einsum(pattern, weights, value_rows, preferred_element_type=jnp.float32)
    weight_sum = jnp.sum(weights.astype(jnp.float32), -1)
    return (summed, weight_sum, peak)


def split_two(values):
    high = values.astype(jnp.bfloat16)
    low = (values - high.astype(jnp.float32)).astype(jnp.bfloat16)
    return [high, low]


def split_three(values):
    high = values.astype(jnp.bfloat16)
    rest = values - high.astype(jnp.float32)
    middle = rest.astype(jnp.bfloat16)
    low = (rest - middle.astype(jnp.float32)).astype(jnp.bfloat16)
    return [high, middle, low]


def join(pieces):
    total = pieces[0].astype(jnp.float32)
    for piece in pieces[1:]:
        total = total + piece.astype(jnp.float32)
    return total


def group_size(axes):
    size = 1
    for axis in axes if isinstance(axes, tuple) else (axes,):
        size = size * lax.axis_size(axis)
    return size


def gather_rows(values, axes):
    count = group_size(axes)
    spread = jnp.broadcast_to(values[None], (count,) + values.shape)
    received = lax.all_to_all(spread, axes, 0, 0, tiled=False)
    return received.reshape(count * values.shape[0], values.shape[1])


def scatter_rows(values, axes):
    count = group_size(axes)
    blocks = values.reshape(count, values.shape[0] // count, values.shape[1])
    received = lax.all_to_all(blocks, axes, 0, 0, tiled=False)
    return jnp.sum(received.astype(jnp.float32), 0).astype(values.dtype)


def local(
    hidden,
    norm_gain,
    w_query,
    w_keyval,
    w_output,
    node_cache,
    leaf_cache,
    leaf_branch,
    branch_root,
    root_owner,
    branch_owner,
    root_len,
    branch_len,
    leaf_len,
):
    head_dim = w_keyval.shape[1] // 2
    local_leaves = hidden.shape[0]
    group = w_query.shape[1] // head_dim
    factor = head_dim ** (-0.5)
    device = (
        lax.axis_index("z") * (lax.axis_size("y") * lax.axis_size("core"))
        + lax.axis_index("y") * lax.axis_size("core")
        + lax.axis_index("core")
    )
    offset = device * local_leaves
    widened = hidden.astype(jnp.float32)
    normed = (
        widened * lax.rsqrt(jnp.mean(widened * widened, -1, keepdims=True) + 1e-05) * norm_gain
    ).astype(jnp.bfloat16)
    branch_ids = jnp.arange(branch_root.shape[0], dtype=jnp.int32)
    root_ids = jnp.arange(root_owner.shape[0], dtype=jnp.int32)
    own_branch = lax.dynamic_slice_in_dim(leaf_branch, offset, local_leaves)
    own_hits = own_branch[:, None] == branch_ids[None, :]
    own_root = jnp.sum(jnp.where(own_hits, branch_root[None, :], 0), 1)
    positions = (
        jnp.sum(jnp.where(own_root[:, None] == root_ids[None, :], root_len[None, :], 0), 1)
        + jnp.sum(jnp.where(own_hits, branch_len[None, :], 0), 1)
        + leaf_len
    )
    raw_query = jnp.dot(normed, w_query, preferred_element_type=jnp.float32).reshape(
        local_leaves, group, head_dim
    )
    queries = rotate(raw_query, positions[:, None]).astype(jnp.bfloat16)
    node_rows = node_cache[0, 0]
    slots = gather_rows(node_rows, ("y", "core")).reshape(
        -1, node_rows.shape[0], node_rows.shape[1]
    )
    queries, slots = lax.optimization_barrier((queries, slots))
    everyone = gather_rows(queries.reshape(local_leaves, group * head_dim), "z")
    raw_entry = jnp.dot(normed, w_keyval, preferred_element_type=jnp.float32)
    new_entry = jnp.concatenate(
        [rotate(raw_entry[:, :head_dim], positions), raw_entry[:, head_dim:]], -1
    ).astype(jnp.bfloat16)
    leaf_rows = leaf_cache[:, 0]
    slot_index = jnp.arange(leaf_rows.shape[1], dtype=jnp.int32)
    appended = jnp.where(
        (slot_index[None, :] == leaf_len[:, None])[:, :, None], new_entry[:, None, :], leaf_rows
    )
    leaf_scores = (
        jnp.einsum(
            "lgd,lkd->lgk", queries, appended[:, :, :head_dim], preferred_element_type=jnp.float32
        )
        * factor
    )
    leaf_usable = (slot_index[None, :] <= leaf_len[:, None])[:, None, :]
    leaf_sum, leaf_weight, leaf_peak = soft_part(
        leaf_scores, leaf_usable, appended[:, :, head_dim:], "lgk,lkd->lgd"
    )

    row_count = everyone.shape[0]
    slot_count = slots.shape[0]
    z_size = lax.axis_size("z")
    my_y_core = device % slot_count
    first_slot = device - my_y_core
    row_branch = lax.dynamic_slice_in_dim(
        leaf_branch.reshape(z_size, slot_count * local_leaves),
        my_y_core * local_leaves,
        local_leaves,
        axis=1,
    ).reshape(row_count)
    slot_ids = first_slot + jnp.arange(slot_count, dtype=jnp.int32)
    branch_root_hits = branch_root[:, None] == root_ids[None, :]
    root_slot_of_branch = jnp.any(
        branch_root_hits[:, None, :] & (root_owner[None, None, :] == slot_ids[None, :, None]), 2
    )
    branch_slot_of_branch = branch_owner[:, None] == slot_ids[None, :]
    row_hits = row_branch[:, None] == branch_ids[None, :]
    root_mine = jnp.any(row_hits[:, :, None] & root_slot_of_branch[None, :, :], 1)
    branch_mine = jnp.any(row_hits[:, :, None] & branch_slot_of_branch[None, :, :], 1)
    mine_all = root_mine | branch_mine
    slot_length = jnp.sum(
        jnp.where(root_owner[None, :] == slot_ids[:, None], root_len[None, :], 0), 1
    ) + jnp.sum(jnp.where(branch_owner[None, :] == slot_ids[:, None], branch_len[None, :], 0), 1)
    node_usable = (
        jnp.arange(slots.shape[1], dtype=jnp.int32)[None, :] < slot_length[:, None]
    )
    rows_query = everyone.reshape(row_count, group, head_dim)
    scores = (
        jnp.einsum(
            "ngd,skd->nsgk", rows_query, slots[:, :, :head_dim], preferred_element_type=jnp.float32
        )
        * factor
    )
    usable = mine_all[:, :, None, None] & node_usable[None, :, None, :]
    slot_sum, slot_weight, slot_peak = soft_part(
        scores, usable, slots[:, :, head_dim:], "nsgk,skd->nsgd"
    )
    slot_peak = jnp.where(mine_all[:, :, None], slot_peak, 0.0)

    def pick(mask, values):
        shape = mask.shape + (1,) * (values.ndim - mask.ndim)
        return jnp.sum(jnp.where(mask.reshape(shape), values, 0.0), 1)

    parts = [
        (pick(mask, slot_sum), pick(mask, slot_weight), pick(mask, slot_peak))
        for mask in (root_mine, branch_mine)
    ]
    pieces = []
    stats = []
    for part_sum, part_weight, part_peak in parts:
        pieces.append(part_sum.reshape(row_count, group * head_dim).astype(jnp.bfloat16))
        stats.append(jnp.concatenate(split_two(part_weight) + split_three(part_peak), -1))
    stat_width = stats[0].shape[1]
    pad_width = (-(2 * group * head_dim + 2 * stat_width)) % 128
    packet = jnp.concatenate(
        pieces + stats + [jnp.zeros((row_count, pad_width), jnp.bfloat16)], -1
    )
    gathered = scatter_rows(packet, "z")
    sums = []
    weights = []
    peaks = []
    for part in range(2):
        sums.append(
            gathered[:, part * group * head_dim : (part + 1) * group * head_dim]
            .astype(jnp.float32)
            .reshape(local_leaves, group, head_dim)
        )
        base = 2 * group * head_dim + part * stat_width
        weights.append(join([gathered[:, base + k * group : base + (k + 1) * group] for k in range(2)]))
        base = base + 2 * group
        peaks.append(join([gathered[:, base + k * group : base + (k + 1) * group] for k in range(3)]))
    sums.append(leaf_sum)
    weights.append(leaf_weight)
    peaks.append(leaf_peak)
    peak = jnp.maximum(jnp.maximum(peaks[0], peaks[1]), peaks[2])
    numerator = jnp.zeros_like(leaf_sum)
    denominator = jnp.zeros_like(leaf_weight)
    for summed, weight_sum, part_peak in zip(sums, weights, peaks):
        scaled = jnp.exp(part_peak - peak)
        numerator = numerator + scaled[..., None] * summed
        denominator = denominator + scaled * weight_sum
    attended = (
        (numerator / denominator[..., None])
        .astype(jnp.bfloat16)
        .reshape(local_leaves, group * head_dim)
    )
    term = jnp.dot(attended, w_output, preferred_element_type=jnp.float32)
    tensor_size = lax.axis_size("tensor")
    pieces = lax.all_to_all(
        term.reshape(local_leaves, tensor_size, term.shape[1] // tensor_size).astype(jnp.bfloat16),
        "tensor",
        1,
        1,
        tiled=False,
    )
    mixed = jnp.sum(pieces.astype(jnp.float32), 1).astype(jnp.bfloat16)
    return (mixed, new_entry[:, None, :])


def solution(mesh):
    tensor_size = mesh.shape["tensor"]
    request_size = mesh.shape["request"]
    core_size = 2
    y_size = 4
    z_size = request_size // (y_size * core_size)
    fine = Mesh(
        mesh.devices.reshape(tensor_size, z_size, y_size, core_size),
        ("tensor", "z", "y", "core"),
    )
    request = ("z", "y", "core")
    in_specs = (
        P(request, None),
        P(),
        P(None, "tensor"),
        P(None, "tensor"),
        P("tensor", None),
        P(request, "tensor", None, None),
        P(request, "tensor", None, None),
        P(),
        P(),
        P(),
        P(),
        P(),
        P(),
        P(request),
    )
    out_specs = (P(request, "tensor"), P(request, "tensor", None))
    return jax.shard_map(local, mesh=fine, in_specs=in_specs, out_specs=out_specs, check_vma=False)
```
